32 devices in a mesh: kv: 8 (over y, x, core), head: 4 (over z).
Axes of the slice: x: 2, y: 2, z: 4, core: 2. Of those that a mesh axis runs over, the one named last changes fastest.
Arguments:
- tokens: bfloat16 [128, 5120], P(None, 'kv'), may hold values from -6 to 6
- q_weight: bfloat16 [5120, 8192], P('kv', 'head'), may hold values from -0.078125 to 0.078125
- key_matrix: bfloat16 [5120, 1024], P('kv', 'head'), may hold values from -0.078125 to 0.078125
- value_matrix: bfloat16 [5120, 1024], P('kv', 'head'), may hold values from -0.078125 to 0.078125
- q_gain: float32 [64, 128], P('head'), may hold values from 0.4 to 45, as said below
- key_norm_scale: float32 [8, 128], P('head'), may hold values from 0.4 to 1.8
- stored_cache_keys: bfloat16 [32, 8192, 8, 128], P(None, 'kv', 'head'), may hold values from -6 to 6
- stored_cache_values: bfloat16 [32, 8192, 8, 128], P(None, 'kv', 'head'), may hold values from -6 to 6
- lengths: int32 [32], replicated, may hold values from 8 to 8192, as said below
- positions: int32 [32, 4], replicated, may hold values from 8 to 8195, as said below
- o_weight: bfloat16 [8192, 5120], P('head', 'kv'), may hold values from -0.0625 to 0.0625
Outputs:
- layer_out: bfloat16 [128, 5120], P('head', 'kv')
The draws below stay inside these ranges and needn't reach their ends.
Inputs may be any that keep to these rules, and one draw needn't show every extreme that they name: `lengths`: every length is 8 or more; one request in each draw has exactly 8192 live positions. positions[r, 0] = lengths[r], and each later draft's position equals the previous one's or exceeds it by one; the request with 8192 live positions has its drafts at consecutive positions. `q_gain`: positive scales.
All inputs are finite; a program needn't handle non-finite values.
Results may differ from the reference program's by a relative error of at most 0.015.
Values may be sent and summed in bfloat16 or wider, within the bound.
No kernel may reach another device: no remote copies, remote signals or barrier semaphores. Data moves between devices by JAX's collectives and lax.ppermute only.
A program may use at most 128 MiB of HBM per device.

```python
import math
import jax
import jax.numpy as jnp
from jax import lax

MODEL_WIDTH = 5120
QUERY_HEADS = 64
KEY_VALUE_HEADS = 8
HEAD_SIZE = 128
DRAFT_TOKENS = 4
REQUEST_COUNT = 32
CACHE_LENGTH = 8192
ROWS = 128


def lengths_and_places(key):
    base = jax.random.fold_in(key, 7)
    key_exp, key_off, key_pick, key_step = jax.random.split(base, 4)
    top_bit = CACHE_LENGTH.bit_length() - 1
    exponent = jax.random.randint(key_exp, (REQUEST_COUNT,), 3, top_bit)
    lowest = jnp.left_shift(jnp.ones((REQUEST_COUNT,), jnp.int32), exponent.astype(jnp.int32))
    length = jax.random.randint(key_off, (REQUEST_COUNT,), lowest, 2 * lowest)
    picked = jax.random.randint(key_pick, (), 0, REQUEST_COUNT)
    chosen = jnp.arange(REQUEST_COUNT) == picked
    length = jnp.where(chosen, CACHE_LENGTH, length).astype(jnp.int32)
    steps = jax.random.randint(key_step, (REQUEST_COUNT, DRAFT_TOKENS - 1), 0, 2)
    steps = jnp.where(chosen[:, None], 1, steps).astype(jnp.int32)
    depth = jnp.concatenate([jnp.zeros((REQUEST_COUNT, 1), jnp.int32), jnp.cumsum(steps, axis=1).astype(jnp.int32)], axis=1)
    return (length, (length[:, None] + depth).astype(jnp.int32))


def draw_lengths(key, part):
    return lengths_and_places(key)[0]


def draw_positions(key, part):
    return lengths_and_places(key)[1]


def draw_q_gain(key, part):
    return jax.random.uniform(key, (QUERY_HEADS, HEAD_SIZE), jnp.float32, 0.4, 1.8)


def level_of(stream_key, dims, shards, least, top_value):
    def one(axis_at, shards_of):
        heights = jax.random.uniform(jax.random.fold_in(jax.random.fold_in(stream_key, 6), axis_at), (shards_of,), jnp.float32, least / len(shards), top_value / len(shards))
        return jnp.repeat(jnp.exp(heights), dims[axis_at] // shards_of).reshape((-1,) + (1,) * (len(dims) - axis_at - 1))

    loudness = one(*shards[0])
    for cut in shards[1:]:
        loudness = loudness * one(*cut)
    return loudness


def bell_draw(stream_key, shape, scale, reach, cuts=(), held_as=jnp.bfloat16):
    level = level_of(stream_key, shape, cuts, -0.22, 0.18) if cuts else 1.0
    entries = jax.random.normal(stream_key, shape, jnp.float32) * scale * level
    return jnp.minimum(jnp.maximum(entries, -reach), reach).astype(held_as)


def setup_inputs(seed: int = 0) -> dict:
    streams_of = jax.random.split(jax.random.key(seed), 12)
    return {
        "tokens": bell_draw(streams_of[0], (ROWS, MODEL_WIDTH), 1.0, 6.0, ((1, 8),)),
        "q_weight": bell_draw(streams_of[1], (MODEL_WIDTH, QUERY_HEADS * HEAD_SIZE), MODEL_WIDTH ** -0.5, 0.078125, ((0, 8), (1, 4))),
        "key_matrix": bell_draw(streams_of[2], (MODEL_WIDTH, KEY_VALUE_HEADS * HEAD_SIZE), MODEL_WIDTH ** -0.5, 0.078125, ((0, 8), (1, 4))),
        "value_matrix": bell_draw(streams_of[3], (MODEL_WIDTH, KEY_VALUE_HEADS * HEAD_SIZE), MODEL_WIDTH ** -0.5, 0.078125, ((0, 8), (1, 4))),
        "q_gain": draw_q_gain(jax.random.fold_in(streams_of[11], 71), 0),
        "key_norm_scale": jnp.clip(0.4 + 1.4 * jax.random.uniform(streams_of[5], (KEY_VALUE_HEADS, HEAD_SIZE), jnp.float32) ** level_of(streams_of[5], (KEY_VALUE_HEADS, HEAD_SIZE), ((0, 4),), -0.2, 0.2), 0.4, 1.8),
        "stored_cache_keys": bell_draw(streams_of[6], (REQUEST_COUNT, CACHE_LENGTH, KEY_VALUE_HEADS, HEAD_SIZE), 1.0, 6.0, ((1, 8), (2, 4))),
        "stored_cache_values": bell_draw(streams_of[7], (REQUEST_COUNT, CACHE_LENGTH, KEY_VALUE_HEADS, HEAD_SIZE), 1.0, 6.0, ((1, 8), (2, 4))),
        "lengths": draw_lengths(jax.random.fold_in(streams_of[11], 71), 0),
        "positions": draw_positions(jax.random.fold_in(streams_of[11], 71), 0),
        "o_weight": bell_draw(streams_of[10], (QUERY_HEADS * HEAD_SIZE, MODEL_WIDTH), (QUERY_HEADS * HEAD_SIZE) ** -0.5, 0.0625, ((0, 4), (1, 8))),
    }


EPSILON = 1e-06
ROPE_BASE = 1000000.0
NEG = -1e+30

def norm_rotate(proj, gain, pos_rows):
    heads, head_dim = gain.shape
    count = proj.shape[0]
    vec = proj.reshape(count, heads, head_dim)
    vec = vec * lax.rsqrt(lax.optimization_barrier(jnp.mean(vec * vec, axis=-1, keepdims=True)) + EPSILON) * gain
    half = head_dim // 2
    freq = ROPE_BASE ** (-(jnp.arange(half, dtype=jnp.float32) * 2.0 / head_dim))
    angle = pos_rows.astype(jnp.float32)[:, None, None] * freq
    cosine = jnp.cos(angle)
    sine = jnp.sin(angle)
    first = vec[..., :half]
    second = vec[..., half:]
    out = jnp.concatenate([first * cosine - second * sine, second * cosine + first * sine], axis=-1)
    return out.reshape(count, heads * head_dim).astype(jnp.bfloat16)

def reference(tokens, q_weight, key_matrix, value_matrix, q_gain, key_norm_scale, stored_cache_keys, stored_cache_values, lengths, positions, o_weight):
    rows = tokens.shape[0]
    pos_rows = positions.reshape(rows)
    query_rows = norm_rotate(jnp.dot(tokens, q_weight, preferred_element_type=jnp.float32), q_gain, pos_rows)
    incoming_keys = norm_rotate(jnp.dot(tokens, key_matrix, preferred_element_type=jnp.float32), key_norm_scale, pos_rows)
    incoming_values = jnp.dot(tokens, value_matrix, preferred_element_type=jnp.float32).astype(jnp.bfloat16)
    group_size = QUERY_HEADS // KEY_VALUE_HEADS
    query_heads_full = query_rows.reshape(REQUEST_COUNT, DRAFT_TOKENS, KEY_VALUE_HEADS, group_size, HEAD_SIZE)
    draft_key_rows = incoming_keys.reshape(REQUEST_COUNT, DRAFT_TOKENS, KEY_VALUE_HEADS, HEAD_SIZE)
    draft_value_rows = incoming_values.reshape(REQUEST_COUNT, DRAFT_TOKENS, KEY_VALUE_HEADS, HEAD_SIZE)

    def one_request(items):
        query, keys, values, new_keys, new_values, length, place = items
        keys_all = jnp.concatenate([keys, new_keys], axis=0).astype(jnp.float32)
        values_all = jnp.concatenate([values, new_values], axis=0).astype(jnp.float32)
        scores = jnp.einsum('jkgd,tkd->jkgt', query.astype(jnp.float32), keys_all, precision=lax.Precision.HIGHEST) / math.sqrt(HEAD_SIZE)
        cache_live = jnp.arange(CACHE_LENGTH, dtype=jnp.int32) < length
        order = jnp.arange(DRAFT_TOKENS, dtype=jnp.int32)
        draft_live = (order[None, :] == order[:, None]) | (order[None, :] < order[:, None]) & (place[None, :] < place[:, None])
        live = jnp.concatenate([jnp.broadcast_to(cache_live[None, :], (DRAFT_TOKENS, CACHE_LENGTH)), draft_live], axis=1)
        mask = live[:, None, None, :]
        top = lax.optimization_barrier(jnp.max(jnp.where(mask, scores, NEG), axis=-1, keepdims=True))
        weights = jnp.where(mask, jnp.exp(scores - top), 0.0)
        total = lax.optimization_barrier(jnp.sum(weights, axis=-1))
        rounded = lax.optimization_barrier(weights.astype(jnp.bfloat16))
        acc = jnp.einsum('jkgt,tkd->jkgd', rounded.astype(jnp.float32), values_all, precision=lax.Precision.HIGHEST)
        return (acc / total[..., None]).astype(jnp.bfloat16)
    attended = lax.map(one_request, (query_heads_full, stored_cache_keys, stored_cache_values, draft_key_rows, draft_value_rows, lengths, positions))
    attended = attended.reshape(rows, QUERY_HEADS * HEAD_SIZE)
    return jnp.dot(attended, o_weight, preferred_element_type=jnp.float32).astype(jnp.bfloat16)
```

```python
import functools
import math

import jax
import jax.numpy as jnp
from jax import lax
from jax.experimental import pallas as pl
from jax.experimental.pallas import tpu as pltpu
from jax.sharding import PartitionSpec as P

EPSILON = 1e-06
ROPE_BASE = 1000000.0
NEG = -1e30


def norm_rotate(proj, gain, pos_rows):
    heads, head_dim = gain.shape
    count = proj.shape[0]
    vec = proj.reshape(count, heads, head_dim)
    vec = vec * lax.rsqrt(jnp.mean(vec * vec, axis=-1, keepdims=True) + EPSILON) * gain
    half = head_dim // 2
    freq = ROPE_BASE ** (-(jnp.arange(half, dtype=jnp.float32) * 2.0 / head_dim))
    angle = pos_rows.astype(jnp.float32)[:, None, None] * freq
    cosine = jnp.cos(angle)
    sine = jnp.sin(angle)
    first = vec[..., :half]
    second = vec[..., half:]
    out = jnp.concatenate([first * cosine - second * sine, second * cosine + first * sine], axis=-1)
    return out.reshape(count, heads * head_dim).astype(jnp.bfloat16)


def log2_exact(value):
    shift = value.bit_length() - 1
    assert (1 << shift) == value
    return shift


def cache_kernel(kreq, kblk, live, q_ref, k_ref, v_ref, acc_out, m_out, l_out, m_sc, l_sc, acc_sc,
                 *, nb, tb, kv_shift, g_shift, scale):
    step = pl.program_id(0)
    req = step // nb
    blk = step % nb

    @pl.when(blk == 0)
    def _():
        m_sc[...] = jnp.full(m_sc.shape, NEG, jnp.float32)
        l_sc[...] = jnp.zeros(l_sc.shape, jnp.float32)
        acc_sc[...] = jnp.zeros(acc_sc.shape, jnp.float32)

    count = live[req]
    start = blk * tb

    @pl.when(start < count)
    def _():
        q = q_ref[0]
        keys = k_ref[0]
        s = lax.dot_general(q, keys, (((1,), (1,)), ((), ())), preferred_element_type=jnp.float32)
        s = s * scale
        col = lax.broadcasted_iota(jnp.int32, s.shape, 1)
        row = lax.broadcasted_iota(jnp.int32, s.shape, 0)
        kv_mask = (1 << kv_shift) - 1
        valid = ((col >> kv_shift) + start < count) & (
            (col & kv_mask) == ((row >> g_shift) & kv_mask)
        )
        s = jnp.where(valid, s, NEG)
        m_prev = m_sc[...]
        m_new = jnp.maximum(m_prev, jnp.max(s, axis=1, keepdims=True))
        alpha = jnp.exp(m_prev - m_new)
        p = jnp.exp(s - m_new)
        l_sc[...] = alpha * l_sc[...] + jnp.sum(p, axis=1, keepdims=True)
        acc_sc[...] = alpha * acc_sc[...] + jnp.dot(
            p.astype(jnp.bfloat16), v_ref[0], preferred_element_type=jnp.float32
        )
        m_sc[...] = m_new

    @pl.when(blk == nb - 1)
    def _():
        acc_out[0] = acc_sc[...]
        m_out[0] = m_sc[...]
        l_out[0] = l_sc[...]


def cache_attention(q_blocks, keys, values, live, kv_local, group_size):
    reqs, rows, head_dim = q_blocks.shape
    flat_len = keys.shape[1]
    local_len = flat_len // kv_local
    tb = min(512, local_len)
    nb = local_len // tb
    steps = reqs * nb
    step_ids = jnp.arange(steps, dtype=jnp.int32)
    step_live = (step_ids % nb) * tb < live[step_ids // nb]
    last_live = lax.cummax(jnp.where(step_live, step_ids, 0), axis=0)
    kreq = last_live // nb
    kblk = last_live % nb
    kernel = functools.partial(
        cache_kernel,
        nb=nb,
        tb=tb,
        kv_shift=log2_exact(kv_local),
        g_shift=log2_exact(group_size),
        scale=1.0 / math.sqrt(head_dim),
    )
    kv_block = tb * kv_local
    grid_spec = pltpu.PrefetchScalarGridSpec(
        num_scalar_prefetch=3,
        grid=(steps,),
        in_specs=[
            pl.BlockSpec((1, rows, head_dim), lambda i, kr, kb, lv: (i // nb, 0, 0)),
            pl.BlockSpec((1, kv_block, head_dim), lambda i, kr, kb, lv: (kr[i], kb[i], 0)),
            pl.BlockSpec((1, kv_block, head_dim), lambda i, kr, kb, lv: (kr[i], kb[i], 0)),
        ],
        out_specs=[
            pl.BlockSpec((1, rows, head_dim), lambda i, kr, kb, lv: (i // nb, 0, 0)),
            pl.BlockSpec((1, rows, 1), lambda i, kr, kb, lv: (i // nb, 0, 0)),
            pl.BlockSpec((1, rows, 1), lambda i, kr, kb, lv: (i // nb, 0, 0)),
        ],
        scratch_shapes=[
            pltpu.VMEM((rows, 1), jnp.float32),
            pltpu.VMEM((rows, 1), jnp.float32),
            pltpu.VMEM((rows, head_dim), jnp.float32),
        ],
    )
    return pl.pallas_call(
        kernel,
        grid_spec=grid_spec,
        out_shape=[
            jax.ShapeDtypeStruct((reqs, rows, head_dim), jnp.float32),
            jax.ShapeDtypeStruct((reqs, rows, 1), jnp.float32),
            jax.ShapeDtypeStruct((reqs, rows, 1), jnp.float32),
        ],
        compiler_params=pltpu.CompilerParams(dimension_semantics=("arbitrary",)),
    )(kreq, kblk, live, q_blocks, keys, values)


def on_device(
    tokens,
    q_weight,
    key_matrix,
    value_matrix,
    q_gain,
    key_norm_scale,
    stored_cache_keys,
    stored_cache_values,
    lengths,
    positions,
    o_weight,
):
    rows = tokens.shape[0]
    reqs, drafts = positions.shape
    kv_size = lax.axis_size("kv")
    kv_idx = lax.axis_index("kv")
    own_rows = rows // kv_size
    own_reqs = own_rows // drafts
    row0 = kv_idx * own_rows
    kv_local, head_dim = key_norm_scale.shape
    heads_local = q_gain.shape[0]
    group_size = heads_local // kv_local

    q_part = jnp.dot(tokens, q_weight, preferred_element_type=jnp.float32)
    k_part = jnp.dot(tokens, key_matrix, preferred_element_type=jnp.float32)
    v_part = jnp.dot(tokens, value_matrix, preferred_element_type=jnp.float32)
    q_own, k_own, v_own = lax.psum_scatter(
        (q_part, k_part, v_part), "kv", scatter_dimension=0, tiled=True
    )
    pos_own = lax.dynamic_slice_in_dim(positions.reshape(rows), row0, own_rows)
    q_own = norm_rotate(q_own, q_gain, pos_own)
    k_own = norm_rotate(k_own, key_norm_scale, pos_own)
    v_own = v_own.astype(jnp.bfloat16)
    query_rows = lax.all_gather(q_own, "kv", axis=0, tiled=True)

    local_len = stored_cache_keys.shape[1]
    offset = kv_idx * local_len
    live = jnp.clip(lengths - offset, 0, local_len).astype(jnp.int32)
    q_blocks = query_rows.reshape(reqs, drafts * heads_local, head_dim)
    keys = stored_cache_keys.reshape(reqs, local_len * kv_local, head_dim)
    values = stored_cache_values.reshape(reqs, local_len * kv_local, head_dim)
    acc_c, m_c, l_c = cache_attention(q_blocks, keys, values, live, kv_local, group_size)
    acc_c = acc_c.reshape(rows, heads_local, head_dim)
    m_c = m_c.reshape(rows, heads_local)
    l_c = l_c.reshape(rows, heads_local)

    scale = 1.0 / math.sqrt(head_dim)
    q_d = q_own.reshape(own_reqs, drafts, kv_local, group_size, head_dim)
    k_d = k_own.reshape(own_reqs, drafts, kv_local, head_dim)
    v_d = v_own.reshape(own_reqs, drafts, kv_local, head_dim)
    s_d = jnp.einsum("rjkgd,rikd->rjkgi", q_d, k_d, preferred_element_type=jnp.float32) * scale
    pos_req = lax.dynamic_slice_in_dim(positions, kv_idx * own_reqs, own_reqs)
    order = jnp.arange(drafts, dtype=jnp.int32)
    seen = (order[None, :] == order[:, None])[None] | (order[None, :] < order[:, None])[None] & (
        pos_req[:, None, :] < pos_req[:, :, None]
    )
    mask_d = seen[:, :, None, None, :]
    s_d = jnp.where(mask_d, s_d, NEG)
    m_d = jnp.max(s_d, axis=-1)
    p_d = jnp.where(mask_d, jnp.exp(s_d - m_d[..., None]), 0.0)
    l_d = jnp.sum(p_d, axis=-1).reshape(own_rows, heads_local)
    acc_d = jnp.einsum(
        "rjkgi,rikd->rjkgd", p_d.astype(jnp.bfloat16), v_d, preferred_element_type=jnp.float32
    ).reshape(own_rows, heads_local, head_dim)
    m_d = m_d.reshape(own_rows, heads_local)

    m_mine = jnp.maximum(lax.dynamic_slice_in_dim(m_c, row0, own_rows), m_d)
    m_all = lax.dynamic_update_slice_in_dim(m_c, m_mine, row0, 0)
    top = lax.pmax(m_all, "kv")
    ratio = jnp.exp(m_c - top)
    acc_s, l_s = lax.psum_scatter(
        (acc_c * ratio[..., None], l_c * ratio), "kv", scatter_dimension=0, tiled=True
    )
    top_own = lax.dynamic_slice_in_dim(top, row0, own_rows)
    ratio_d = jnp.exp(m_d - top_own)
    acc_s = acc_s + acc_d * ratio_d[..., None]
    l_s = l_s + l_d * ratio_d
    attended = (acc_s / l_s[..., None]).astype(jnp.bfloat16).reshape(own_rows, heads_local * head_dim)
    attended = lax.all_gather(attended, "kv", axis=0, tiled=True)
    return lax.psum_scatter(
        jnp.dot(attended, o_weight, preferred_element_type=jnp.float32).astype(jnp.bfloat16),
        "head",
        scatter_dimension=0,
        tiled=True,
    )


def solution(mesh):
    placed = (
        P(None, "kv"),
        P("kv", "head"),
        P("kv", "head"),
        P("kv", "head"),
        P("head", None),
        P("head", None),
        P(None, "kv", "head", None),
        P(None, "kv", "head", None),
        P(),
        P(),
        P("head", "kv"),
    )
    return jax.shard_map(
        on_device, mesh=mesh, in_specs=placed, out_specs=P("head", "kv"), check_vma=False
    )
```

```python
import functools
import math

import jax
import jax.numpy as jnp
from jax import lax
from jax.experimental import pallas as pl
from jax.experimental.pallas import tpu as pltpu
from jax.sharding import PartitionSpec as P

EPSILON = 1e-06
ROPE_BASE = 1000000.0
NEG = -1e30


def norm_rotate(proj, gain, pos_rows):
    heads, head_dim = gain.shape
    count = proj.shape[0]
    vec = proj.reshape(count, heads, head_dim)
    vec = vec * lax.rsqrt(jnp.mean(vec * vec, axis=-1, keepdims=True) + EPSILON) * gain
    half = head_dim // 2
    freq = ROPE_BASE ** (-(jnp.arange(half, dtype=jnp.float32) * 2.0 / head_dim))
    angle = pos_rows.astype(jnp.float32)[:, None, None] * freq
    cosine = jnp.cos(angle)
    sine = jnp.sin(angle)
    first = vec[..., :half]
    second = vec[..., half:]
    out = jnp.concatenate([first * cosine - second * sine, second * cosine + first * sine], axis=-1)
    return out.reshape(count, heads * head_dim).astype(jnp.bfloat16)


def log2_exact(value):
    shift = value.bit_length() - 1
    assert (1 << shift) == value
    return shift


def cache_kernel(kgrp, live, q_ref, k_ref, v_ref, acc_out, m_out, l_out,
                 *, rb, chunk, kv_shift, g_shift, scale):
    step = pl.program_id(0)
    rows = q_ref.shape[1]
    width = chunk << kv_shift
    kv_mask = (1 << kv_shift) - 1
    col = lax.broadcasted_iota(jnp.int32, (rows, width), 1)
    row = lax.broadcasted_iota(jnp.int32, (rows, width), 0)
    same_head = (col & kv_mask) == ((row >> g_shift) & kv_mask)
    col_pos = col >> kv_shift
    for slot in range(rb):
        count = live[step * rb + slot]
        q = q_ref[slot]

        def body(c, carry):
            m_prev, l_prev, acc_prev = carry
            base = pl.multiple_of(c * width, width)
            keys = k_ref[slot, pl.ds(base, width), :]
            s = lax.dot_general(q, keys, (((1,), (1,)), ((), ())), preferred_element_type=jnp.float32)
            s = s * scale
            valid = same_head & (col_pos + c * chunk < count)
            s = jnp.where(valid, s, NEG)
            m_new = jnp.maximum(m_prev, jnp.max(s, axis=1, keepdims=True))
            alpha = jnp.exp(m_prev - m_new)
            p = jnp.exp(s - m_new)
            l_new = alpha * l_prev + jnp.sum(p, axis=1, keepdims=True)
            acc_new = alpha * acc_prev + jnp.dot(
                p.astype(jnp.bfloat16), v_ref[slot, pl.ds(base, width), :],
                preferred_element_type=jnp.float32,
            )
            return m_new, l_new, acc_new

        init = (
            jnp.full((rows, 1), NEG, jnp.float32),
            jnp.zeros((rows, 1), jnp.float32),
            jnp.zeros((rows, q_ref.shape[2]), jnp.float32),
        )
        m, l, acc = lax.fori_loop(0, (count + chunk - 1) // chunk, body, init)
        acc_out[slot] = acc
        m_out[slot] = m
        l_out[slot] = l


def cache_attention(q_blocks, keys, values, live, kv_local, group_size):
    reqs, rows, head_dim = q_blocks.shape
    flat_len = keys.shape[1]
    local_len = flat_len // kv_local
    chunk = min(256, local_len)
    rb = 2 if reqs % 2 == 0 else 1
    steps = reqs // rb
    step_ids = jnp.arange(steps, dtype=jnp.int32)
    step_live = jnp.max(live.reshape(steps, rb), axis=1) > 0
    kgrp = lax.cummax(jnp.where(step_live, step_ids, 0), axis=0)
    kernel = functools.partial(
        cache_kernel,
        rb=rb,
        chunk=chunk,
        kv_shift=log2_exact(kv_local),
        g_shift=log2_exact(group_size),
        scale=1.0 / math.sqrt(head_dim),
    )
    grid_spec = pltpu.PrefetchScalarGridSpec(
        num_scalar_prefetch=2,
        grid=(steps,),
        in_specs=[
            pl.BlockSpec((rb, rows, head_dim), lambda i, kg, lv: (i, 0, 0)),
            pl.BlockSpec((rb, flat_len, head_dim), lambda i, kg, lv: (kg[i], 0, 0)),
            pl.BlockSpec((rb, flat_len, head_dim), lambda i, kg, lv: (kg[i], 0, 0)),
        ],
        out_specs=[
            pl.BlockSpec((rb, rows, head_dim), lambda i, kg, lv: (i, 0, 0)),
            pl.BlockSpec((rb, rows, 1), lambda i, kg, lv: (i, 0, 0)),
            pl.BlockSpec((rb, rows, 1), lambda i, kg, lv: (i, 0, 0)),
        ],
    )
    return pl.pallas_call(
        kernel,
        grid_spec=grid_spec,
        out_shape=[
            jax.ShapeDtypeStruct((reqs, rows, head_dim), jnp.float32),
            jax.ShapeDtypeStruct((reqs, rows, 1), jnp.float32),
            jax.ShapeDtypeStruct((reqs, rows, 1), jnp.float32),
        ],
        compiler_params=pltpu.CompilerParams(dimension_semantics=("arbitrary",)),
    )(kgrp, live, q_blocks, keys, values)


def sum_over(part, axis):
    size = lax.axis_size(axis)
    split = part.reshape((size, part.shape[0] // size) + part.shape[1:])
    return jnp.sum(lax.all_to_all(split, axis, 0, 0).astype(jnp.float32), axis=0)


def on_device(
    tokens,
    q_weight,
    key_matrix,
    value_matrix,
    q_gain,
    key_norm_scale,
    stored_cache_keys,
    stored_cache_values,
    lengths,
    positions,
    o_weight,
):
    rows = tokens.shape[0]
    reqs, drafts = positions.shape
    kv_size = lax.axis_size("kv")
    kv_idx = lax.axis_index("kv")
    own_rows = rows // kv_size
    own_reqs = own_rows // drafts
    row0 = kv_idx * own_rows
    kv_local, head_dim = key_norm_scale.shape
    heads_local = q_gain.shape[0]
    group_size = heads_local // kv_local
    q_width = heads_local * head_dim
    k_width = kv_local * head_dim

    proj = jnp.concatenate(
        [
            jnp.dot(tokens, q_weight, preferred_element_type=jnp.float32),
            jnp.dot(tokens, key_matrix, preferred_element_type=jnp.float32),
            jnp.dot(tokens, value_matrix, preferred_element_type=jnp.float32),
        ],
        axis=1,
    )
    proj_own = sum_over(proj, "kv")
    pos_own = lax.dynamic_slice_in_dim(positions.reshape(rows), row0, own_rows)
    q_own = norm_rotate(proj_own[:, :q_width], q_gain, pos_own)
    k_own = norm_rotate(proj_own[:, q_width:q_width + k_width], key_norm_scale, pos_own)
    v_own = proj_own[:, q_width + k_width:].astype(jnp.bfloat16)
    query_rows = lax.all_gather(q_own, "kv", axis=0, tiled=True)

    local_len = stored_cache_keys.shape[1]
    offset = kv_idx * local_len
    live = jnp.clip(lengths - offset, 0, local_len).astype(jnp.int32)
    q_blocks = query_rows.reshape(reqs, drafts * heads_local, head_dim)
    keys = stored_cache_keys.reshape(reqs, local_len * kv_local, head_dim)
    values = stored_cache_values.reshape(reqs, local_len * kv_local, head_dim)
    acc_c, m_c, l_c = cache_attention(q_blocks, keys, values, live, kv_local, group_size)
    stat_pad = max(128, 2 * heads_local)
    packed = jnp.concatenate(
        [
            acc_c.reshape(rows, q_width),
            m_c.reshape(rows, heads_local),
            l_c.reshape(rows, heads_local),
            jnp.zeros((rows, stat_pad - 2 * heads_local), jnp.float32),
        ],
        axis=1,
    )
    packed = packed.reshape(kv_size, own_rows, q_width + stat_pad)
    gathered = lax.all_to_all(packed, "kv", 0, 0)
    acc_g = gathered[:, :, :q_width].reshape(kv_size, own_rows, heads_local, head_dim)
    m_g = gathered[:, :, q_width:q_width + heads_local]
    l_g = gathered[:, :, q_width + heads_local:q_width + 2 * heads_local]

    scale = 1.0 / math.sqrt(head_dim)
    q_d = q_own.reshape(own_reqs, drafts, kv_local, group_size, head_dim)
    k_d = k_own.reshape(own_reqs, drafts, kv_local, head_dim)
    v_d = v_own.reshape(own_reqs, drafts, kv_local, head_dim)
    s_d = jnp.einsum("rjkgd,rikd->rjkgi", q_d, k_d, preferred_element_type=jnp.float32) * scale
    pos_req = lax.dynamic_slice_in_dim(positions, kv_idx * own_reqs, own_reqs)
    order = jnp.arange(drafts, dtype=jnp.int32)
    seen = (order[None, :] == order[:, None])[None] | (order[None, :] < order[:, None])[None] & (
        pos_req[:, None, :] < pos_req[:, :, None]
    )
    mask_d = seen[:, :, None, None, :]
    s_d = jnp.where(mask_d, s_d, NEG)
    m_d = jnp.max(s_d, axis=-1)
    p_d = jnp.where(mask_d, jnp.exp(s_d - m_d[..., None]), 0.0)
    l_d = jnp.sum(p_d, axis=-1).reshape(own_rows, heads_local)
    acc_d = jnp.einsum(
        "rjkgi,rikd->rjkgd", p_d.astype(jnp.bfloat16), v_d, preferred_element_type=jnp.float32
    ).reshape(own_rows, heads_local, head_dim)
    m_d = m_d.reshape(own_rows, heads_local)

    top = jnp.maximum(jnp.max(m_g, axis=0), m_d)
    ratio = jnp.exp(m_g - top[None])
    ratio_d = jnp.exp(m_d - top)
    total = jnp.sum(l_g * ratio, axis=0) + l_d * ratio_d
    acc = jnp.sum(acc_g * ratio[..., None], axis=0) + acc_d * ratio_d[..., None]
    attended = (acc / total[..., None]).astype(jnp.bfloat16).reshape(own_rows, q_width)
    attended = lax.all_gather(attended, "kv", axis=0, tiled=True)
    partial_out = jnp.dot(attended, o_weight, preferred_element_type=jnp.float32)
    return sum_over(partial_out.astype(jnp.bfloat16), "head").astype(jnp.bfloat16)


def solution(mesh):
    placed = (
        P(None, "kv"),
        P("kv", "head"),
        P("kv", "head"),
        P("kv", "head"),
        P("head", None),
        P("head", None),
        P(None, "kv", "head", None),
        P(None, "kv", "head", None),
        P(),
        P(),
        P("head", "kv"),
    )
    return jax.shard_map(
        on_device, mesh=mesh, in_specs=placed, out_specs=P("head", "kv"), check_vma=False
    )
```

```python
import functools
import math

import jax
import jax.numpy as jnp
from jax import lax
from jax.experimental import pallas as pl
from jax.experimental.pallas import tpu as pltpu
from jax.sharding import PartitionSpec as P

EPSILON = 1e-06
ROPE_BASE = 1000000.0
NEG = -1e30


def norm_rotate(proj, gain, pos_rows):
    heads, head_dim = gain.shape
    count = proj.shape[0]
    vec = proj.reshape(count, heads, head_dim)
    vec = vec * lax.rsqrt(jnp.mean(vec * vec, axis=-1, keepdims=True) + EPSILON) * gain
    half = head_dim // 2
    freq = ROPE_BASE ** (-(jnp.arange(half, dtype=jnp.float32) * 2.0 / head_dim))
    angle = pos_rows.astype(jnp.float32)[:, None, None] * freq
    cosine = jnp.cos(angle)
    sine = jnp.sin(angle)
    first = vec[..., :half]
    second = vec[..., half:]
    out = jnp.concatenate([first * cosine - second * sine, second * cosine + first * sine], axis=-1)
    return out.reshape(count, heads * head_dim).astype(jnp.bfloat16)


def log2_exact(value):
    shift = value.bit_length() - 1
    assert (1 << shift) == value
    return shift


def cache_kernel(kgrp, live, q_ref, k_ref, v_ref, out_ref,
                 *, rb, chunk, kv_shift, g_shift, scale):
    step = pl.program_id(0)
    rows = q_ref.shape[1]
    width = chunk << kv_shift
    kv_mask = (1 << kv_shift) - 1
    col = lax.broadcasted_iota(jnp.int32, (rows, width), 1)
    row = lax.broadcasted_iota(jnp.int32, (rows, width), 0)
    same_head = (col & kv_mask) == ((row >> g_shift) & kv_mask)
    col_pos = col >> kv_shift
    lanes = out_ref.shape[2]
    for slot in range(rb):
        count = live[step * rb + slot]
        q = q_ref[slot]

        def body(c, carry):
            m_prev, l_prev, acc_prev = carry
            base = pl.multiple_of(c * width, width)
            keys = k_ref[slot, pl.ds(base, width), :]
            s = lax.dot_general(q, keys, (((1,), (1,)), ((), ())), preferred_element_type=jnp.float32)
            s = s * scale
            valid = same_head & (col_pos + c * chunk < count)
            s = jnp.where(valid, s, NEG)
            m_new = jnp.maximum(m_prev, jnp.max(s, axis=1, keepdims=True))
            alpha = jnp.exp(m_prev - m_new)
            p = jnp.exp(s - m_new)
            l_new = alpha * l_prev + jnp.sum(p, axis=1, keepdims=True)
            acc_new = alpha * acc_prev + jnp.dot(
                p.astype(jnp.bfloat16), v_ref[slot, pl.ds(base, width), :],
                preferred_element_type=jnp.float32,
            )
            return m_new, l_new, acc_new

        init = (
            jnp.full((rows, 1), NEG, jnp.float32),
            jnp.zeros((rows, 1), jnp.float32),
            jnp.zeros((rows, q_ref.shape[2]), jnp.float32),
        )
        m, l, acc = lax.fori_loop(0, (count + chunk - 1) // chunk, body, init)
        out_ref[slot, :rows, :] = acc
        pieces = [jnp.broadcast_to(m, (rows, lanes)), jnp.broadcast_to(l, (rows, lanes))]
        if lanes > 2 * rows:
            pieces.append(jnp.zeros((lanes - 2 * rows, lanes), jnp.float32))
        stacked = jnp.concatenate(pieces, axis=0)
        out_ref[slot, rows:, :] = jnp.transpose(stacked)[: out_ref.shape[1] - rows, :]


def cache_attention(q_blocks, keys, values, live, kv_local, group_size):
    reqs, rows, head_dim = q_blocks.shape
    assert 2 * rows <= head_dim
    flat_len = keys.shape[1]
    local_len = flat_len // kv_local
    chunk = min(256, local_len)
    rb = 2 if reqs % 2 == 0 else 1
    steps = reqs // rb
    step_ids = jnp.arange(steps, dtype=jnp.int32)
    step_live = jnp.max(live.reshape(steps, rb), axis=1) > 0
    kgrp = lax.cummax(jnp.where(step_live, step_ids, 0), axis=0)
    kernel = functools.partial(
        cache_kernel,
        rb=rb,
        chunk=chunk,
        kv_shift=log2_exact(kv_local),
        g_shift=log2_exact(group_size),
        scale=1.0 / math.sqrt(head_dim),
    )
    out_rows = rows + 8
    grid_spec = pltpu.PrefetchScalarGridSpec(
        num_scalar_prefetch=2,
        grid=(steps,),
        in_specs=[
            pl.BlockSpec((rb, rows, head_dim), lambda i, kg, lv: (i, 0, 0)),
            pl.BlockSpec((rb, flat_len, head_dim), lambda i, kg, lv: (kg[i], 0, 0)),
            pl.BlockSpec((rb, flat_len, head_dim), lambda i, kg, lv: (kg[i], 0, 0)),
        ],
        out_specs=pl.BlockSpec((rb, out_rows, head_dim), lambda i, kg, lv: (i, 0, 0)),
    )
    return pl.pallas_call(
        kernel,
        grid_spec=grid_spec,
        out_shape=jax.ShapeDtypeStruct((reqs, out_rows, head_dim), jnp.float32),
        compiler_params=pltpu.CompilerParams(dimension_semantics=("arbitrary",)),
    )(kgrp, live, q_blocks, keys, values)


def sum_over(part, axis):
    size = lax.axis_size(axis)
    split = part.reshape((size, part.shape[0] // size) + part.shape[1:])
    return jnp.sum(lax.all_to_all(split, axis, 0, 0).astype(jnp.float32), axis=0)


def on_device(
    tokens,
    q_weight,
    key_matrix,
    value_matrix,
    q_gain,
    key_norm_scale,
    stored_cache_keys,
    stored_cache_values,
    lengths,
    positions,
    o_weight,
):
    rows = tokens.shape[0]
    reqs, drafts = positions.shape
    kv_size = lax.axis_size("kv")
    kv_idx = lax.axis_index("kv")
    own_rows = rows // kv_size
    own_reqs = own_rows // drafts
    row0 = kv_idx * own_rows
    kv_local, head_dim = key_norm_scale.shape
    heads_local = q_gain.shape[0]
    group_size = heads_local // kv_local
    q_width = heads_local * head_dim
    k_width = kv_local * head_dim

    proj = jnp.concatenate(
        [
            jnp.dot(tokens, q_weight, preferred_element_type=jnp.float32),
            jnp.dot(tokens, key_matrix, preferred_element_type=jnp.float32),
            jnp.dot(tokens, value_matrix, preferred_element_type=jnp.float32),
        ],
        axis=1,
    )
    proj_own = sum_over(proj, "kv")
    pos_own = lax.dynamic_slice_in_dim(positions.reshape(rows), row0, own_rows)
    q_own = norm_rotate(proj_own[:, :q_width], q_gain, pos_own)
    k_own = norm_rotate(proj_own[:, q_width:q_width + k_width], key_norm_scale, pos_own)
    v_own = proj_own[:, q_width + k_width:].astype(jnp.bfloat16)
    rows_r = drafts * heads_local
    q_blocks = lax.all_gather(
        q_own.reshape(own_reqs, rows_r, head_dim), "kv", axis=0, tiled=True
    )

    local_len = stored_cache_keys.shape[1]
    offset = kv_idx * local_len
    live = jnp.clip(lengths - offset, 0, local_len).astype(jnp.int32)
    keys = stored_cache_keys.reshape(reqs, local_len * kv_local, head_dim)
    values = stored_cache_values.reshape(reqs, local_len * kv_local, head_dim)
    partial = cache_attention(q_blocks, keys, values, live, kv_local, group_size)
    gathered = lax.all_to_all(
        partial.reshape((kv_size, own_reqs) + partial.shape[1:]), "kv", 0, 0
    )
    acc_g = gathered[:, :, :rows_r, :]
    m_g = gathered[:, :, rows_r, :rows_r]
    l_g = gathered[:, :, rows_r, rows_r:2 * rows_r]

    scale = 1.0 / math.sqrt(head_dim)
    q_d = q_own.reshape(own_reqs, drafts, kv_local, group_size, head_dim)
    k_d = k_own.reshape(own_reqs, drafts, kv_local, head_dim)
    v_d = v_own.reshape(own_reqs, drafts, kv_local, head_dim)
    s_d = jnp.einsum("rjkgd,rikd->rjkgi", q_d, k_d, preferred_element_type=jnp.float32) * scale
    pos_req = lax.dynamic_slice_in_dim(positions, kv_idx * own_reqs, own_reqs)
    order = jnp.arange(drafts, dtype=jnp.int32)
    seen = (order[None, :] == order[:, None])[None] | (order[None, :] < order[:, None])[None] & (
        pos_req[:, None, :] < pos_req[:, :, None]
    )
    mask_d = seen[:, :, None, None, :]
    s_d = jnp.where(mask_d, s_d, NEG)
    m_d = jnp.max(s_d, axis=-1)
    p_d = jnp.where(mask_d, jnp.exp(s_d - m_d[..., None]), 0.0)
    l_d = jnp.sum(p_d, axis=-1).reshape(own_reqs, rows_r)
    acc_d = jnp.einsum(
        "rjkgi,rikd->rjkgd", p_d.astype(jnp.bfloat16), v_d, preferred_element_type=jnp.float32
    ).reshape(own_reqs, rows_r, head_dim)
    m_d = m_d.reshape(own_reqs, rows_r)

    top = jnp.maximum(jnp.max(m_g, axis=0), m_d)
    ratio = jnp.exp(m_g - top[None])
    ratio_d = jnp.exp(m_d - top)
    total = jnp.sum(l_g * ratio, axis=0) + l_d * ratio_d
    acc = jnp.sum(acc_g * ratio[..., None], axis=0) + acc_d * ratio_d[..., None]
    attended = (acc / total[..., None]).astype(jnp.bfloat16).reshape(own_rows, q_width)
    attended = lax.all_gather(attended, "kv", axis=0, tiled=True)
    partial_out = jnp.dot(attended, o_weight, preferred_element_type=jnp.float32)
    return sum_over(partial_out.astype(jnp.bfloat16), "head").astype(jnp.bfloat16)


def solution(mesh):
    placed = (
        P(None, "kv"),
        P("kv", "head"),
        P("kv", "head"),
        P("kv", "head"),
        P("head", None),
        P("head", None),
        P(None, "kv", "head", None),
        P(None, "kv", "head", None),
        P(),
        P(),
        P("head", "kv"),
    )
    return jax.shard_map(
        on_device, mesh=mesh, in_specs=placed, out_specs=P("head", "kv"), check_vma=False
    )
```

```python
import functools
import math

import jax
import jax.numpy as jnp
from jax import lax
from jax.experimental import pallas as pl
from jax.experimental.pallas import tpu as pltpu
from jax.sharding import PartitionSpec as P

EPSILON = 1e-06
ROPE_BASE = 1000000.0
NEG = -1e30


def norm_rotate(proj, gain, pos_rows):
    heads, head_dim = gain.shape
    count = proj.shape[0]
    vec = proj.reshape(count, heads, head_dim)
    vec = vec * lax.rsqrt(jnp.mean(vec * vec, axis=-1, keepdims=True) + EPSILON) * gain
    half = head_dim // 2
    freq = ROPE_BASE ** (-(jnp.arange(half, dtype=jnp.float32) * 2.0 / head_dim))
    angle = pos_rows.astype(jnp.float32)[:, None, None] * freq
    cosine = jnp.cos(angle)
    sine = jnp.sin(angle)
    first = vec[..., :half]
    second = vec[..., half:]
    out = jnp.concatenate([first * cosine - second * sine, second * cosine + first * sine], axis=-1)
    return out.reshape(count, heads * head_dim).astype(jnp.bfloat16)


def log2_exact(value):
    shift = value.bit_length() - 1
    assert (1 << shift) == value
    return shift


def attend_chunks(items, chunk, trips, kv_shift, g_shift, scale):
    rows = items[0][0].shape[0]
    head_dim = items[0][0].shape[1]
    width = chunk << kv_shift
    kv_mask = (1 << kv_shift) - 1
    col = lax.broadcasted_iota(jnp.int32, (rows, width), 1)
    row = lax.broadcasted_iota(jnp.int32, (rows, width), 0)
    same_head = (col & kv_mask) == ((row >> g_shift) & kv_mask)
    col_pos = col >> kv_shift

    def one(c, item, carry):
        q, kbuf, vbuf, count = item
        m_prev, l_prev, acc_prev = carry
        base = pl.multiple_of(c * width, width)
        keys = kbuf[pl.ds(base, width), :]
        s = lax.dot_general(q, keys, (((1,), (1,)), ((), ())), preferred_element_type=jnp.float32)
        s = s * scale
        valid = same_head & (col_pos + c * chunk < count)
        s = jnp.where(valid, s, NEG)
        m_new = jnp.maximum(m_prev, jnp.max(s, axis=1, keepdims=True))
        alpha = jnp.exp(m_prev - m_new)
        p = jnp.exp(s - m_new)
        l_new = alpha * l_prev + jnp.sum(p, axis=1, keepdims=True)
        acc_new = alpha * acc_prev + jnp.dot(
            p.astype(jnp.bfloat16), vbuf[pl.ds(base, width), :], preferred_element_type=jnp.float32
        )
        return m_new, l_new, acc_new

    def body(c, carries):
        return tuple(one(c, item, carry) for item, carry in zip(items, carries))

    init = tuple(
        (
            jnp.full((rows, 1), NEG, jnp.float32),
            jnp.zeros((rows, 1), jnp.float32),
            jnp.zeros((rows, head_dim), jnp.float32),
        )
        for _ in items
    )
    if isinstance(trips, int) and trips == 1:
        return body(0, init)
    return lax.fori_loop(0, trips, body, init)


def cache_kernel(live, q_ref, k_hbm, v_hbm, out_ref, kbuf, vbuf, sems,
                 *, sub, kv_shift, g_shift, scale):
    reqs, rows, head_dim = q_ref.shape
    group = kbuf.shape[1]
    flat_len = kbuf.shape[2]
    sub_rows = sub << kv_shift
    subs = flat_len // sub_rows
    lanes = out_ref.shape[2]
    local_len = flat_len >> kv_shift
    vbuf[...] = jnp.zeros(vbuf.shape, vbuf.dtype)

    def copies(first, slot):
        out = []
        for member in range(group):
            for c in range(subs):
                window = pl.ds(c * sub_rows, sub_rows)
                out.append((
                    member,
                    c,
                    pltpu.make_async_copy(k_hbm.at[first + member, window, :],
                                          kbuf.at[slot, member, window, :], sems.at[slot, member, 0, c]),
                    pltpu.make_async_copy(v_hbm.at[first + member, window, :],
                                          vbuf.at[slot, member, window, :], sems.at[slot, member, 1, c]),
                ))
        return out

    def start(first, slot):
        for member, c, kc, vc in copies(first, slot):
            @pl.when(c * sub < live[first + member])
            def _():
                kc.start()
                vc.start()

    def wait(first, slot):
        for member, c, kc, vc in copies(first, slot):
            @pl.when(c * sub < live[first + member])
            def _():
                kc.wait()
                vc.wait()

    start(0, 0)
    small = min(sub, local_len)
    mid = min(2 * sub, local_len)
    big = min(4 * sub, local_len)

    def per_group(index, carry):
        slot = index % 2
        first = index * group

        @pl.when(first + group < reqs)
        def _():
            start(first + group, 1 - slot)

        wait(first, slot)
        counts = [live[first + member] for member in range(group)]
        top = counts[0]
        for count in counts[1:]:
            top = jnp.maximum(top, count)
        items = [
            (q_ref[first + member], kbuf.at[slot, member], vbuf.at[slot, member], counts[member])
            for member in range(group)
        ]

        def finish(results):
            for member, (m, l, acc) in enumerate(results):
                alive = counts[member] > 0
                m = jnp.where(alive, m, NEG)
                l = jnp.where(alive, l, 0.0)
                acc = jnp.where(alive, acc, 0.0)
                out_ref[first + member, :rows, :] = acc
                pieces = [jnp.broadcast_to(m, (rows, lanes)), jnp.broadcast_to(l, (rows, lanes))]
                if lanes > 2 * rows:
                    pieces.append(jnp.zeros((lanes - 2 * rows, lanes), jnp.float32))
                stacked = jnp.concatenate(pieces, axis=0)
                out_ref[first + member, rows:, :] = jnp.transpose(stacked)[: out_ref.shape[1] - rows, :]

        @pl.when(top == 0)
        def _():
            finish([
                (
                    jnp.full((rows, 1), NEG, jnp.float32),
                    jnp.zeros((rows, 1), jnp.float32),
                    jnp.zeros((rows, head_dim), jnp.float32),
                )
                for _ in range(group)
            ])

        @pl.when((top > 0) & (top <= small))
        def _():
            finish(attend_chunks(items, small, 1, kv_shift, g_shift, scale))

        @pl.when((top > small) & (top <= mid))
        def _():
            finish(attend_chunks(items, mid, 1, kv_shift, g_shift, scale))

        @pl.when(top > mid)
        def _():
            finish(attend_chunks(items, big, (top + big - 1) // big, kv_shift, g_shift, scale))

        return carry

    lax.fori_loop(0, reqs // group, per_group, 0)


def cache_attention(q_blocks, keys, values, live, kv_local, group_size, sub=256, group=4):
    reqs, rows, head_dim = q_blocks.shape
    assert 2 * rows <= head_dim
    flat_len = keys.shape[1]
    local_len = flat_len // kv_local
    sub = min(sub, local_len)
    assert local_len % (4 * sub) == 0 or local_len <= 4 * sub
    group = group if reqs % group == 0 else 1
    kernel = functools.partial(
        cache_kernel,
        sub=sub,
        kv_shift=log2_exact(kv_local),
        g_shift=log2_exact(group_size),
        scale=1.0 / math.sqrt(head_dim),
    )
    vmem = pltpu.MemorySpace.VMEM if hasattr(pltpu, "MemorySpace") else pltpu.TPUMemorySpace.VMEM
    return pl.pallas_call(
        kernel,
        in_specs=[
            pl.BlockSpec(memory_space=pltpu.SMEM),
            pl.BlockSpec(memory_space=vmem),
            pl.BlockSpec(memory_space=pl.ANY),
            pl.BlockSpec(memory_space=pl.ANY),
        ],
        out_specs=pl.BlockSpec(memory_space=vmem),
        out_shape=jax.ShapeDtypeStruct((reqs, rows + 8, head_dim), jnp.float32),
        scratch_shapes=[
            pltpu.VMEM((2, group, flat_len, head_dim), keys.dtype),
            pltpu.VMEM((2, group, flat_len, head_dim), values.dtype),
            pltpu.SemaphoreType.DMA((2, group, 2, flat_len // (sub * kv_local))),
        ],
    )(live, q_blocks, keys, values)


def sum_over(part, axis):
    size = lax.axis_size(axis)
    split = part.reshape((size, part.shape[0] // size) + part.shape[1:])
    return jnp.sum(lax.all_to_all(split, axis, 0, 0).astype(jnp.float32), axis=0)


def on_device(
    tokens,
    q_weight,
    key_matrix,
    value_matrix,
    q_gain,
    key_norm_scale,
    stored_cache_keys,
    stored_cache_values,
    lengths,
    positions,
    o_weight,
):
    rows = tokens.shape[0]
    reqs, drafts = positions.shape
    kv_size = lax.axis_size("kv")
    kv_idx = lax.axis_index("kv")
    own_rows = rows // kv_size
    own_reqs = own_rows // drafts
    row0 = kv_idx * own_rows
    kv_local, head_dim = key_norm_scale.shape
    heads_local = q_gain.shape[0]
    group_size = heads_local // kv_local
    q_width = heads_local * head_dim
    k_width = kv_local * head_dim

    proj = jnp.concatenate(
        [
            jnp.dot(tokens, q_weight, preferred_element_type=jnp.float32),
            jnp.dot(tokens, key_matrix, preferred_element_type=jnp.float32),
            jnp.dot(tokens, value_matrix, preferred_element_type=jnp.float32),
        ],
        axis=1,
    )
    proj_own = sum_over(proj, "kv")
    pos_own = lax.dynamic_slice_in_dim(positions.reshape(rows), row0, own_rows)
    q_own = norm_rotate(proj_own[:, :q_width], q_gain, pos_own)
    k_own = norm_rotate(proj_own[:, q_width:q_width + k_width], key_norm_scale, pos_own)
    v_own = proj_own[:, q_width + k_width:].astype(jnp.bfloat16)
    rows_r = drafts * heads_local
    q_blocks = lax.all_gather(
        q_own.reshape(own_reqs, rows_r, head_dim), "kv", axis=0, tiled=True
    )

    local_len = stored_cache_keys.shape[1]
    offset = kv_idx * local_len
    live = jnp.clip(lengths - offset, 0, local_len).astype(jnp.int32)
    keys = stored_cache_keys.reshape(reqs, local_len * kv_local, head_dim)
    values = stored_cache_values.reshape(reqs, local_len * kv_local, head_dim)
    partial = cache_attention(q_blocks, keys, values, live, kv_local, group_size)
    gathered = lax.all_to_all(
        partial.reshape((kv_size, own_reqs) + partial.shape[1:]), "kv", 0, 0
    )
    acc_g = gathered[:, :, :rows_r, :]
    m_g = gathered[:, :, rows_r, :rows_r]
    l_g = gathered[:, :, rows_r, rows_r:2 * rows_r]

    scale = 1.0 / math.sqrt(head_dim)
    q_d = q_own.reshape(own_reqs, drafts, kv_local, group_size, head_dim)
    k_d = k_own.reshape(own_reqs, drafts, kv_local, head_dim)
    v_d = v_own.reshape(own_reqs, drafts, kv_local, head_dim)
    s_d = jnp.einsum("rjkgd,rikd->rjkgi", q_d, k_d, preferred_element_type=jnp.float32) * scale
    pos_req = lax.dynamic_slice_in_dim(positions, kv_idx * own_reqs, own_reqs)
    order = jnp.arange(drafts, dtype=jnp.int32)
    seen = (order[None, :] == order[:, None])[None] | (order[None, :] < order[:, None])[None] & (
        pos_req[:, None, :] < pos_req[:, :, None]
    )
    mask_d = seen[:, :, None, None, :]
    s_d = jnp.where(mask_d, s_d, NEG)
    m_d = jnp.max(s_d, axis=-1)
    p_d = jnp.where(mask_d, jnp.exp(s_d - m_d[..., None]), 0.0)
    l_d = jnp.sum(p_d, axis=-1).reshape(own_reqs, rows_r)
    acc_d = jnp.einsum(
        "rjkgi,rikd->rjkgd", p_d.astype(jnp.bfloat16), v_d, preferred_element_type=jnp.float32
    ).reshape(own_reqs, rows_r, head_dim)
    m_d = m_d.reshape(own_reqs, rows_r)

    top = jnp.maximum(jnp.max(m_g, axis=0), m_d)
    ratio = jnp.exp(m_g - top[None])
    ratio_d = jnp.exp(m_d - top)
    total = jnp.sum(l_g * ratio, axis=0) + l_d * ratio_d
    acc = jnp.sum(acc_g * ratio[..., None], axis=0) + acc_d * ratio_d[..., None]
    attended = (acc / total[..., None]).astype(jnp.bfloat16).reshape(own_rows, q_width)
    attended = lax.all_gather(attended, "kv", axis=0, tiled=True)
    partial_out = jnp.dot(attended, o_weight, preferred_element_type=jnp.float32)
    return sum_over(partial_out.astype(jnp.bfloat16), "head").astype(jnp.bfloat16)


def solution(mesh):
    placed = (
        P(None, "kv"),
        P("kv", "head"),
        P("kv", "head"),
        P("kv", "head"),
        P("head", None),
        P("head", None),
        P(None, "kv", "head", None),
        P(None, "kv", "head", None),
        P(),
        P(),
        P("head", "kv"),
    )
    return jax.shard_map(
        on_device, mesh=mesh, in_specs=placed, out_specs=P("head", "kv"), check_vma=False
    )
```

```python
import functools
import math

import jax
import jax.numpy as jnp
from jax import lax
from jax.experimental import pallas as pl
from jax.experimental.pallas import tpu as pltpu
from jax.sharding import PartitionSpec as P

EPSILON = 1e-06
ROPE_BASE = 1000000.0
NEG = -1e30


def norm_rotate(proj, gain, pos_rows):
    heads, head_dim = gain.shape
    count = proj.shape[0]
    vec = proj.reshape(count, heads, head_dim)
    vec = vec * lax.rsqrt(jnp.mean(vec * vec, axis=-1, keepdims=True) + EPSILON) * gain
    half = head_dim // 2
    freq = ROPE_BASE ** (-(jnp.arange(half, dtype=jnp.float32) * 2.0 / head_dim))
    angle = pos_rows.astype(jnp.float32)[:, None, None] * freq
    cosine = jnp.cos(angle)
    sine = jnp.sin(angle)
    first = vec[..., :half]
    second = vec[..., half:]
    out = jnp.concatenate([first * cosine - second * sine, second * cosine + first * sine], axis=-1)
    return out.reshape(count, heads * head_dim).astype(jnp.bfloat16)


def log2_exact(value):
    shift = value.bit_length() - 1
    assert (1 << shift) == value
    return shift


def split_pieces(value, count):
    pieces = []
    rest = value
    for _ in range(count):
        piece = rest.astype(jnp.bfloat16).astype(jnp.float32)
        pieces.append(piece)
        rest = rest - piece
    return pieces


def stat_groups(vectors, per_row):
    return [vectors[i:i + per_row] for i in range(0, len(vectors), per_row)]


def attend_chunks(items, chunk, trips, kv_shift, g_shift, scale):
    rows = items[0][0].shape[0]
    head_dim = items[0][0].shape[1]
    width = chunk << kv_shift
    kv_mask = (1 << kv_shift) - 1
    col = lax.broadcasted_iota(jnp.int32, (rows, width), 1)
    row = lax.broadcasted_iota(jnp.int32, (rows, width), 0)
    same_head = (col & kv_mask) == ((row >> g_shift) & kv_mask)
    col_pos = col >> kv_shift

    def one(c, item, carry):
        q, kbuf, vbuf, count = item
        m_prev, l_prev, acc_prev = carry
        base = pl.multiple_of(c * width, width)
        keys = kbuf[pl.ds(base, width), :]
        s = lax.dot_general(q, keys, (((1,), (1,)), ((), ())), preferred_element_type=jnp.float32)
        s = s * scale
        valid = same_head & (col_pos + c * chunk < count)
        s = jnp.where(valid, s, NEG)
        m_new = jnp.maximum(m_prev, jnp.max(s, axis=1, keepdims=True))
        alpha = jnp.exp(m_prev - m_new)
        p = jnp.exp(s - m_new)
        l_new = alpha * l_prev + jnp.sum(p, axis=1, keepdims=True)
        acc_new = alpha * acc_prev + jnp.dot(
            p.astype(jnp.bfloat16), vbuf[pl.ds(base, width), :], preferred_element_type=jnp.float32
        )
        return m_new, l_new, acc_new

    def body(c, carries):
        return tuple(one(c, item, carry) for item, carry in zip(items, carries))

    init = tuple(
        (
            jnp.full((rows, 1), NEG, jnp.float32),
            jnp.zeros((rows, 1), jnp.float32),
            jnp.zeros((rows, head_dim), jnp.float32),
        )
        for _ in items
    )
    if isinstance(trips, int) and trips == 1:
        return body(0, init)
    return lax.fori_loop(0, trips, body, init)


def cache_kernel(live, q_ref, k_hbm, v_hbm, out_ref, kbuf, vbuf, sems,
                 *, sub, kv_shift, g_shift, scale):
    reqs, rows, head_dim = q_ref.shape
    group = kbuf.shape[1]
    flat_len = kbuf.shape[2]
    sub_rows = sub << kv_shift
    subs = flat_len // sub_rows
    lanes = out_ref.shape[2]
    local_len = flat_len >> kv_shift
    vbuf[...] = jnp.zeros(vbuf.shape, vbuf.dtype)

    def copies(first, slot):
        out = []
        for member in range(group):
            for c in range(subs):
                window = pl.ds(c * sub_rows, sub_rows)
                out.append((
                    member,
                    c,
                    pltpu.make_async_copy(k_hbm.at[first + member, window, :],
                                          kbuf.at[slot, member, window, :], sems.at[slot, member, 0, c]),
                    pltpu.make_async_copy(v_hbm.at[first + member, window, :],
                                          vbuf.at[slot, member, window, :], sems.at[slot, member, 1, c]),
                ))
        return out

    def start(first, slot):
        for member, c, kc, vc in copies(first, slot):
            @pl.when(c * sub < live[first + member])
            def _():
                kc.start()
                vc.start()

    def wait(first, slot):
        for member, c, kc, vc in copies(first, slot):
            @pl.when(c * sub < live[first + member])
            def _():
                kc.wait()
                vc.wait()

    start(0, 0)
    small = min(sub, local_len)
    mid = min(2 * sub, local_len)
    big = min(4 * sub, local_len)

    def per_group(index, carry):
        slot = index % 2
        first = index * group

        @pl.when(first + group < reqs)
        def _():
            start(first + group, 1 - slot)

        wait(first, slot)
        counts = [live[first + member] for member in range(group)]
        top = counts[0]
        for count in counts[1:]:
            top = jnp.maximum(top, count)
        items = [
            (q_ref[first + member], kbuf.at[slot, member], vbuf.at[slot, member], counts[member])
            for member in range(group)
        ]

        def finish(results):
            for member, (m, l, acc) in enumerate(results):
                alive = counts[member] > 0
                m = jnp.where(alive, m, NEG)
                l = jnp.where(alive, l, 0.0)
                acc = jnp.where(alive, acc / jnp.where(alive, l, 1.0), 0.0)
                out_ref[first + member, :rows, :] = acc.astype(out_ref.dtype)
                stat_rows = [jnp.zeros((1, lanes), jnp.float32)] * (out_ref.shape[1] - rows)
                for at, piece_group in enumerate(stat_groups(split_pieces(m, 3) + split_pieces(l, 2), lanes // rows)):
                    pieces = [jnp.broadcast_to(v, (rows, lanes)) for v in piece_group]
                    if lanes > rows * len(piece_group):
                        pieces.append(jnp.zeros((lanes - rows * len(piece_group), lanes), jnp.float32))
                    stat_rows[at] = jnp.transpose(jnp.concatenate(pieces, axis=0))[:1, :]
                out_ref[first + member, rows:, :] = jnp.concatenate(stat_rows, axis=0).astype(out_ref.dtype)

        @pl.when(top == 0)
        def _():
            finish([
                (
                    jnp.full((rows, 1), NEG, jnp.float32),
                    jnp.zeros((rows, 1), jnp.float32),
                    jnp.zeros((rows, head_dim), jnp.float32),
                )
                for _ in range(group)
            ])

        @pl.when((top > 0) & (top <= small))
        def _():
            finish(attend_chunks(items, small, 1, kv_shift, g_shift, scale))

        @pl.when((top > small) & (top <= mid))
        def _():
            finish(attend_chunks(items, mid, 1, kv_shift, g_shift, scale))

        @pl.when(top > mid)
        def _():
            finish(attend_chunks(items, big, (top + big - 1) // big, kv_shift, g_shift, scale))

        return carry

    lax.fori_loop(0, reqs // group, per_group, 0)


def cache_attention(q_blocks, keys, values, live, kv_local, group_size, sub=256, group=4):
    reqs, rows, head_dim = q_blocks.shape
    assert 2 * rows <= head_dim
    flat_len = keys.shape[1]
    local_len = flat_len // kv_local
    sub = min(sub, local_len)
    assert local_len % (4 * sub) == 0 or local_len <= 4 * sub
    group = group if reqs % group == 0 else 1
    kernel = functools.partial(
        cache_kernel,
        sub=sub,
        kv_shift=log2_exact(kv_local),
        g_shift=log2_exact(group_size),
        scale=1.0 / math.sqrt(head_dim),
    )
    vmem = pltpu.MemorySpace.VMEM if hasattr(pltpu, "MemorySpace") else pltpu.TPUMemorySpace.VMEM
    return pl.pallas_call(
        kernel,
        in_specs=[
            pl.BlockSpec(memory_space=pltpu.SMEM),
            pl.BlockSpec(memory_space=vmem),
            pl.BlockSpec(memory_space=pl.ANY),
            pl.BlockSpec(memory_space=pl.ANY),
        ],
        out_specs=pl.BlockSpec(memory_space=vmem),
        out_shape=jax.ShapeDtypeStruct((reqs, rows + 16, head_dim), jnp.bfloat16),
        scratch_shapes=[
            pltpu.VMEM((2, group, flat_len, head_dim), keys.dtype),
            pltpu.VMEM((2, group, flat_len, head_dim), values.dtype),
            pltpu.SemaphoreType.DMA((2, group, 2, flat_len // (sub * kv_local))),
        ],
    )(live, q_blocks, keys, values)


def sum_over(part, axis):
    size = lax.axis_size(axis)
    split = part.reshape((size, part.shape[0] // size) + part.shape[1:])
    return jnp.sum(lax.all_to_all(split, axis, 0, 0).astype(jnp.float32), axis=0)


def on_device(
    tokens,
    q_weight,
    key_matrix,
    value_matrix,
    q_gain,
    key_norm_scale,
    stored_cache_keys,
    stored_cache_values,
    lengths,
    positions,
    o_weight,
):
    rows = tokens.shape[0]
    reqs, drafts = positions.shape
    kv_size = lax.axis_size("kv")
    kv_idx = lax.axis_index("kv")
    own_rows = rows // kv_size
    own_reqs = own_rows // drafts
    row0 = kv_idx * own_rows
    kv_local, head_dim = key_norm_scale.shape
    heads_local = q_gain.shape[0]
    group_size = heads_local // kv_local
    q_width = heads_local * head_dim
    k_width = kv_local * head_dim

    proj = jnp.concatenate(
        [
            jnp.dot(tokens, q_weight, preferred_element_type=jnp.float32),
            jnp.dot(tokens, key_matrix, preferred_element_type=jnp.float32),
            jnp.dot(tokens, value_matrix, preferred_element_type=jnp.float32),
        ],
        axis=1,
    )
    proj_own = sum_over(proj.astype(jnp.bfloat16), "kv")
    pos_own = lax.dynamic_slice_in_dim(positions.reshape(rows), row0, own_rows)
    q_own = norm_rotate(proj_own[:, :q_width], q_gain, pos_own)
    k_own = norm_rotate(proj_own[:, q_width:q_width + k_width], key_norm_scale, pos_own)
    v_own = proj_own[:, q_width + k_width:].astype(jnp.bfloat16)
    rows_r = drafts * heads_local
    q_blocks = lax.all_gather(
        q_own.reshape(own_reqs, rows_r, head_dim), "kv", axis=0, tiled=True
    )

    local_len = stored_cache_keys.shape[1]
    offset = kv_idx * local_len
    live = jnp.clip(lengths - offset, 0, local_len).astype(jnp.int32)
    keys = stored_cache_keys.reshape(reqs, local_len * kv_local, head_dim)
    values = stored_cache_values.reshape(reqs, local_len * kv_local, head_dim)
    partial = cache_attention(q_blocks, keys, values, live, kv_local, group_size)
    gathered = lax.all_to_all(
        partial.reshape((kv_size, own_reqs) + partial.shape[1:]), "kv", 0, 0
    )
    acc_g = gathered[:, :, :rows_r, :].astype(jnp.float32)
    per_row = head_dim // rows_r
    stats = gathered[:, :, rows_r:, :].astype(jnp.float32)

    def stat(k):
        lane0 = (k % per_row) * rows_r
        return stats[:, :, k // per_row, lane0:lane0 + rows_r]

    m_g = stat(0) + stat(1) + stat(2)
    l_g = stat(3) + stat(4)

    scale = 1.0 / math.sqrt(head_dim)
    q_d = q_own.reshape(own_reqs, drafts, kv_local, group_size, head_dim)
    k_d = k_own.reshape(own_reqs, drafts, kv_local, head_dim)
    v_d = v_own.reshape(own_reqs, drafts, kv_local, head_dim)
    s_d = jnp.einsum("rjkgd,rikd->rjkgi", q_d, k_d, preferred_element_type=jnp.float32) * scale
    pos_req = lax.dynamic_slice_in_dim(positions, kv_idx * own_reqs, own_reqs)
    order = jnp.arange(drafts, dtype=jnp.int32)
    seen = (order[None, :] == order[:, None])[None] | (order[None, :] < order[:, None])[None] & (
        pos_req[:, None, :] < pos_req[:, :, None]
    )
    mask_d = seen[:, :, None, None, :]
    s_d = jnp.where(mask_d, s_d, NEG)
    m_d = jnp.max(s_d, axis=-1)
    p_d = jnp.where(mask_d, jnp.exp(s_d - m_d[..., None]), 0.0)
    l_d = jnp.sum(p_d, axis=-1).reshape(own_reqs, rows_r)
    acc_d = jnp.einsum(
        "rjkgi,rikd->rjkgd", p_d.astype(jnp.bfloat16), v_d, preferred_element_type=jnp.float32
    ).reshape(own_reqs, rows_r, head_dim)
    m_d = m_d.reshape(own_reqs, rows_r)

    top = jnp.maximum(jnp.max(m_g, axis=0), m_d)
    ratio = jnp.exp(m_g - top[None]) * l_g
    ratio_d = jnp.exp(m_d - top)
    total = jnp.sum(ratio, axis=0) + l_d * ratio_d
    acc = jnp.sum(acc_g * ratio[..., None], axis=0) + acc_d * ratio_d[..., None]
    attended = (acc / total[..., None]).astype(jnp.bfloat16).reshape(own_rows, q_width)
    attended = lax.all_gather(attended, "kv", axis=0, tiled=True)
    partial_out = jnp.dot(attended, o_weight, preferred_element_type=jnp.float32)
    return sum_over(partial_out.astype(jnp.bfloat16), "head").astype(jnp.bfloat16)


def solution(mesh):
    placed = (
        P(None, "kv"),
        P("kv", "head"),
        P("kv", "head"),
        P("kv", "head"),
        P("head", None),
        P("head", None),
        P(None, "kv", "head", None),
        P(None, "kv", "head", None),
        P(),
        P(),
        P("head", "kv"),
    )
    return jax.shard_map(
        on_device, mesh=mesh, in_specs=placed, out_specs=P("head", "kv"), check_vma=False
    )
```

```python
import functools
import math

import jax
import jax.numpy as jnp
from jax import lax
from jax.experimental import pallas as pl
from jax.experimental.pallas import tpu as pltpu
from jax.sharding import PartitionSpec as P

EPSILON = 1e-06
ROPE_BASE = 1000000.0
NEG = -1e30


def norm_rotate(proj, gain, pos_rows):
    heads, head_dim = gain.shape
    count = proj.shape[0]
    vec = proj.reshape(count, heads, head_dim)
    vec = vec * lax.rsqrt(jnp.mean(vec * vec, axis=-1, keepdims=True) + EPSILON) * gain
    half = head_dim // 2
    freq = ROPE_BASE ** (-(jnp.arange(half, dtype=jnp.float32) * 2.0 / head_dim))
    angle = pos_rows.astype(jnp.float32)[:, None, None] * freq
    cosine = jnp.cos(angle)
    sine = jnp.sin(angle)
    first = vec[..., :half]
    second = vec[..., half:]
    out = jnp.concatenate([first * cosine - second * sine, second * cosine + first * sine], axis=-1)
    return out.reshape(count, heads * head_dim).astype(jnp.bfloat16)


def log2_exact(value):
    shift = value.bit_length() - 1
    assert (1 << shift) == value
    return shift


def split_pieces(value, count):
    pieces = []
    rest = value
    for _ in range(count):
        piece = rest.astype(jnp.bfloat16).astype(jnp.float32)
        pieces.append(piece)
        rest = rest - piece
    return pieces


def stat_groups(vectors, per_row):
    return [vectors[i:i + per_row] for i in range(0, len(vectors), per_row)]


def attend_chunks(items, chunk, trips, kv_shift, g_shift, scale):
    rows = items[0][0].shape[0]
    head_dim = items[0][0].shape[1]
    width = chunk << kv_shift
    kv_mask = (1 << kv_shift) - 1
    col = lax.broadcasted_iota(jnp.int32, (rows, width), 1)
    row = lax.broadcasted_iota(jnp.int32, (rows, width), 0)
    same_head = (col & kv_mask) == ((row >> g_shift) & kv_mask)
    col_pos = col >> kv_shift

    def one(c, item, carry):
        q, kbuf, vbuf, count = item
        m_prev, l_prev, acc_prev = carry
        base = pl.multiple_of(c * width, width)
        keys = kbuf[pl.ds(base, width), :]
        s = lax.dot_general(q, keys, (((1,), (1,)), ((), ())), preferred_element_type=jnp.float32)
        s = s * scale
        valid = same_head & (col_pos + c * chunk < count)
        s = jnp.where(valid, s, NEG)
        m_new = jnp.maximum(m_prev, jnp.max(s, axis=1, keepdims=True))
        alpha = jnp.exp(m_prev - m_new)
        p = jnp.exp(s - m_new)
        l_new = alpha * l_prev + jnp.sum(p, axis=1, keepdims=True)
        acc_new = alpha * acc_prev + jnp.dot(
            p.astype(jnp.bfloat16), vbuf[pl.ds(base, width), :], preferred_element_type=jnp.float32
        )
        return m_new, l_new, acc_new

    def body(c, carries):
        return tuple(one(c, item, carry) for item, carry in zip(items, carries))

    init = tuple(
        (
            jnp.full((rows, 1), NEG, jnp.float32),
            jnp.zeros((rows, 1), jnp.float32),
            jnp.zeros((rows, head_dim), jnp.float32),
        )
        for _ in items
    )
    if isinstance(trips, int) and trips == 1:
        return body(0, init)
    return lax.fori_loop(0, trips, body, init)


def cache_kernel(order, live, q_ref, k_hbm, v_hbm, out_ref, kbuf, vbuf, sems,
                 *, sub, kv_shift, g_shift, scale):
    reqs, rows, head_dim = q_ref.shape
    group = kbuf.shape[1]
    flat_len = kbuf.shape[2]
    sub_rows = sub << kv_shift
    subs = flat_len // sub_rows
    lanes = out_ref.shape[2]
    local_len = flat_len >> kv_shift

    small = min(sub, local_len)
    mid = min(2 * sub, local_len)
    big = min(4 * sub, local_len)

    def group_of(first):
        members = [order[first + member] for member in range(group)]
        counts = [live[req] for req in members]
        top = counts[0]
        for count in counts[1:]:
            top = jnp.maximum(top, count)
        span = jnp.where(top <= small, small, jnp.where(top <= mid, mid, ((top + big - 1) // big) * big))
        span = jnp.where(top > 0, span, 0)
        return members, counts, top, span

    def copies(first, slot):
        members, _, _, span = group_of(first)
        out = []
        for member in range(group):
            for c in range(subs):
                window = pl.ds(c * sub_rows, sub_rows)
                out.append((
                    c * sub < span,
                    pltpu.make_async_copy(k_hbm.at[members[member], window, :],
                                          kbuf.at[slot, member, window, :], sems.at[slot, member, 0, c]),
                    pltpu.make_async_copy(v_hbm.at[members[member], window, :],
                                          vbuf.at[slot, member, window, :], sems.at[slot, member, 1, c]),
                ))
        return out

    def start(first, slot):
        for needed, kc, vc in copies(first, slot):
            @pl.when(needed)
            def _():
                kc.start()
                vc.start()

    def wait(first, slot):
        for needed, kc, vc in copies(first, slot):
            @pl.when(needed)
            def _():
                kc.wait()
                vc.wait()

    start(0, 0)

    def per_group(index, carry):
        slot = index % 2
        first = index * group

        @pl.when(first + group < reqs)
        def _():
            start(first + group, 1 - slot)

        wait(first, slot)
        members, counts, top, _ = group_of(first)
        items = [
            (q_ref[members[member]], kbuf.at[slot, member], vbuf.at[slot, member], counts[member])
            for member in range(group)
        ]

        def finish(results):
            for member, (m, l, acc) in enumerate(results):
                alive = counts[member] > 0
                m = jnp.where(alive, m, NEG)
                l = jnp.where(alive, l, 0.0)
                acc = jnp.where(alive, acc / jnp.where(alive, l, 1.0), 0.0)
                out_ref[members[member], :rows, :] = acc.astype(out_ref.dtype)
                stat_rows = [jnp.zeros((1, lanes), jnp.float32)] * (out_ref.shape[1] - rows)
                for at, piece_group in enumerate(stat_groups(split_pieces(m, 3) + split_pieces(l, 2), lanes // rows)):
                    pieces = [jnp.broadcast_to(v, (rows, lanes)) for v in piece_group]
                    if lanes > rows * len(piece_group):
                        pieces.append(jnp.zeros((lanes - rows * len(piece_group), lanes), jnp.float32))
                    stat_rows[at] = jnp.transpose(jnp.concatenate(pieces, axis=0))[:1, :]
                out_ref[members[member], rows:, :] = jnp.concatenate(stat_rows, axis=0).astype(out_ref.dtype)

        @pl.when(top == 0)
        def _():
            finish([
                (
                    jnp.full((rows, 1), NEG, jnp.float32),
                    jnp.zeros((rows, 1), jnp.float32),
                    jnp.zeros((rows, head_dim), jnp.float32),
                )
                for _ in range(group)
            ])

        @pl.when((top > 0) & (top <= small))
        def _():
            finish(attend_chunks(items, small, 1, kv_shift, g_shift, scale))

        @pl.when((top > small) & (top <= mid))
        def _():
            finish(attend_chunks(items, mid, 1, kv_shift, g_shift, scale))

        @pl.when(top > mid)
        def _():
            finish(attend_chunks(items, big, (top + big - 1) // big, kv_shift, g_shift, scale))

        return carry

    lax.fori_loop(0, reqs // group, per_group, 0)


def cache_attention(q_blocks, keys, values, live, kv_local, group_size, sub=256, group=4):
    reqs, rows, head_dim = q_blocks.shape
    assert 2 * rows <= head_dim
    flat_len = keys.shape[1]
    local_len = flat_len // kv_local
    sub = min(sub, local_len)
    assert local_len % (4 * sub) == 0 or local_len <= 4 * sub
    group = group if reqs % group == 0 else 1
    kernel = functools.partial(
        cache_kernel,
        sub=sub,
        kv_shift=log2_exact(kv_local),
        g_shift=log2_exact(group_size),
        scale=1.0 / math.sqrt(head_dim),
    )
    ids = jnp.arange(reqs, dtype=jnp.int32)
    sort_key = live * reqs + ids
    rank = jnp.sum((sort_key[None, :] < sort_key[:, None]).astype(jnp.int32), axis=1)
    order = jnp.sum(jnp.where(rank[None, :] == ids[:, None], ids[None, :], 0), axis=1).astype(jnp.int32)
    vmem = pltpu.MemorySpace.VMEM if hasattr(pltpu, "MemorySpace") else pltpu.TPUMemorySpace.VMEM
    return pl.pallas_call(
        kernel,
        in_specs=[
            pl.BlockSpec(memory_space=pltpu.SMEM),
            pl.BlockSpec(memory_space=pltpu.SMEM),
            pl.BlockSpec(memory_space=vmem),
            pl.BlockSpec(memory_space=pl.ANY),
            pl.BlockSpec(memory_space=pl.ANY),
        ],
        out_specs=pl.BlockSpec(memory_space=vmem),
        out_shape=jax.ShapeDtypeStruct((reqs, rows + 16, head_dim), jnp.bfloat16),
        scratch_shapes=[
            pltpu.VMEM((2, group, flat_len, head_dim), keys.dtype),
            pltpu.VMEM((2, group, flat_len, head_dim), values.dtype),
            pltpu.SemaphoreType.DMA((2, group, 2, flat_len // (sub * kv_local))),
        ],
    )(order, live, q_blocks, keys, values)


def sum_over(part, axis):
    size = lax.axis_size(axis)
    split = part.reshape((size, part.shape[0] // size) + part.shape[1:])
    return jnp.sum(lax.all_to_all(split, axis, 0, 0).astype(jnp.float32), axis=0)


def on_device(
    tokens,
    q_weight,
    key_matrix,
    value_matrix,
    q_gain,
    key_norm_scale,
    stored_cache_keys,
    stored_cache_values,
    lengths,
    positions,
    o_weight,
):
    rows = tokens.shape[0]
    reqs, drafts = positions.shape
    kv_size = lax.axis_size("kv")
    kv_idx = lax.axis_index("kv")
    own_rows = rows // kv_size
    own_reqs = own_rows // drafts
    row0 = kv_idx * own_rows
    kv_local, head_dim = key_norm_scale.shape
    heads_local = q_gain.shape[0]
    group_size = heads_local // kv_local
    q_width = heads_local * head_dim
    k_width = kv_local * head_dim

    proj = jnp.concatenate(
        [
            jnp.dot(tokens, q_weight, preferred_element_type=jnp.float32),
            jnp.dot(tokens, key_matrix, preferred_element_type=jnp.float32),
            jnp.dot(tokens, value_matrix, preferred_element_type=jnp.float32),
        ],
        axis=1,
    )
    proj_own = sum_over(proj.astype(jnp.bfloat16), "kv")
    pos_own = lax.dynamic_slice_in_dim(positions.reshape(rows), row0, own_rows)
    q_own = norm_rotate(proj_own[:, :q_width], q_gain, pos_own)
    k_own = norm_rotate(proj_own[:, q_width:q_width + k_width], key_norm_scale, pos_own)
    v_own = proj_own[:, q_width + k_width:].astype(jnp.bfloat16)
    rows_r = drafts * heads_local
    q_blocks = lax.all_gather(
        q_own.reshape(own_reqs, rows_r, head_dim), "kv", axis=0, tiled=True
    )

    local_len = stored_cache_keys.shape[1]
    offset = kv_idx * local_len
    live = jnp.clip(lengths - offset, 0, local_len).astype(jnp.int32)
    keys = stored_cache_keys.reshape(reqs, local_len * kv_local, head_dim)
    values = stored_cache_values.reshape(reqs, local_len * kv_local, head_dim)
    partial = cache_attention(q_blocks, keys, values, live, kv_local, group_size)
    gathered = lax.all_to_all(
        partial.reshape((kv_size, own_reqs) + partial.shape[1:]), "kv", 0, 0
    )
    acc_g = gathered[:, :, :rows_r, :].astype(jnp.float32)
    per_row = head_dim // rows_r
    stats = gathered[:, :, rows_r:, :].astype(jnp.float32)

    def stat(k):
        lane0 = (k % per_row) * rows_r
        return stats[:, :, k // per_row, lane0:lane0 + rows_r]

    m_g = stat(0) + stat(1) + stat(2)
    l_g = stat(3) + stat(4)

    scale = 1.0 / math.sqrt(head_dim)
    q_d = q_own.reshape(own_reqs, drafts, kv_local, group_size, head_dim)
    k_d = k_own.reshape(own_reqs, drafts, kv_local, head_dim)
    v_d = v_own.reshape(own_reqs, drafts, kv_local, head_dim)
    s_d = jnp.einsum("rjkgd,rikd->rjkgi", q_d, k_d, preferred_element_type=jnp.float32) * scale
    pos_req = lax.dynamic_slice_in_dim(positions, kv_idx * own_reqs, own_reqs)
    order = jnp.arange(drafts, dtype=jnp.int32)
    seen = (order[None, :] == order[:, None])[None] | (order[None, :] < order[:, None])[None] & (
        pos_req[:, None, :] < pos_req[:, :, None]
    )
    mask_d = seen[:, :, None, None, :]
    s_d = jnp.where(mask_d, s_d, NEG)
    m_d = jnp.max(s_d, axis=-1)
    p_d = jnp.where(mask_d, jnp.exp(s_d - m_d[..., None]), 0.0)
    l_d = jnp.sum(p_d, axis=-1).reshape(own_reqs, rows_r)
    acc_d = jnp.einsum(
        "rjkgi,rikd->rjkgd", p_d.astype(jnp.bfloat16), v_d, preferred_element_type=jnp.float32
    ).reshape(own_reqs, rows_r, head_dim)
    m_d = m_d.reshape(own_reqs, rows_r)

    top = jnp.maximum(jnp.max(m_g, axis=0), m_d)
    ratio = jnp.exp(m_g - top[None]) * l_g
    ratio_d = jnp.exp(m_d - top)
    total = jnp.sum(ratio, axis=0) + l_d * ratio_d
    acc = jnp.sum(acc_g * ratio[..., None], axis=0) + acc_d * ratio_d[..., None]
    attended = (acc / total[..., None]).astype(jnp.bfloat16).reshape(own_rows, q_width)
    attended = lax.all_gather(attended, "kv", axis=0, tiled=True)
    partial_out = jnp.dot(attended, o_weight, preferred_element_type=jnp.float32)
    return sum_over(partial_out.astype(jnp.bfloat16), "head").astype(jnp.bfloat16)


def solution(mesh):
    placed = (
        P(None, "kv"),
        P("kv", "head"),
        P("kv", "head"),
        P("kv", "head"),
        P("head", None),
        P("head", None),
        P(None, "kv", "head", None),
        P(None, "kv", "head", None),
        P(),
        P(),
        P("head", "kv"),
    )
    return jax.shard_map(
        on_device, mesh=mesh, in_specs=placed, out_specs=P("head", "kv"), check_vma=False
    )
```

```python
import functools
import math

import jax
import jax.numpy as jnp
from jax import lax
from jax.experimental import pallas as pl
from jax.experimental.pallas import tpu as pltpu
from jax.sharding import PartitionSpec as P

EPSILON = 1e-06
ROPE_BASE = 1000000.0
NEG = -1e30


def norm_rotate(proj, gain, pos_rows):
    heads, head_dim = gain.shape
    count = proj.shape[0]
    vec = proj.reshape(count, heads, head_dim)
    vec = vec * lax.rsqrt(jnp.mean(vec * vec, axis=-1, keepdims=True) + EPSILON) * gain
    half = head_dim // 2
    freq = ROPE_BASE ** (-(jnp.arange(half, dtype=jnp.float32) * 2.0 / head_dim))
    angle = pos_rows.astype(jnp.float32)[:, None, None] * freq
    cosine = jnp.cos(angle)
    sine = jnp.sin(angle)
    first = vec[..., :half]
    second = vec[..., half:]
    out = jnp.concatenate([first * cosine - second * sine, second * cosine + first * sine], axis=-1)
    return out.reshape(count, heads * head_dim).astype(jnp.bfloat16)


def log2_exact(value):
    shift = value.bit_length() - 1
    assert (1 << shift) == value
    return shift


def split_pieces(value, count):
    pieces = []
    rest = value
    for _ in range(count):
        piece = rest.astype(jnp.bfloat16).astype(jnp.float32)
        pieces.append(piece)
        rest = rest - piece
    return pieces


def stat_groups(vectors, per_row):
    return [vectors[i:i + per_row] for i in range(0, len(vectors), per_row)]


def attend_chunks(items, chunk, trips, kv_shift, g_shift, scale):
    rows = items[0][0].shape[0]
    head_dim = items[0][0].shape[1]
    width = chunk << kv_shift
    kv_mask = (1 << kv_shift) - 1
    col = lax.broadcasted_iota(jnp.int32, (rows, width), 1)
    row = lax.broadcasted_iota(jnp.int32, (rows, width), 0)
    same_head = (col & kv_mask) == ((row >> g_shift) & kv_mask)
    col_pos = col >> kv_shift

    def one(c, item, carry):
        q, kbuf, vbuf, count = item
        m_prev, l_prev, acc_prev = carry
        base = pl.multiple_of(c * width, width)
        keys = kbuf[pl.ds(base, width), :]
        s = lax.dot_general(q, keys, (((1,), (1,)), ((), ())), preferred_element_type=jnp.float32)
        s = s * scale
        valid = same_head & (col_pos + c * chunk < count)
        s = jnp.where(valid, s, NEG)
        m_new = jnp.maximum(m_prev, jnp.max(s, axis=1, keepdims=True))
        alpha = jnp.exp(m_prev - m_new)
        p = jnp.exp(s - m_new)
        l_new = alpha * l_prev + jnp.sum(p, axis=1, keepdims=True)
        acc_new = alpha * acc_prev + jnp.dot(
            p.astype(jnp.bfloat16), vbuf[pl.ds(base, width), :], preferred_element_type=jnp.float32
        )
        return m_new, l_new, acc_new

    def body(c, carries):
        return tuple(one(c, item, carry) for item, carry in zip(items, carries))

    init = tuple(
        (
            jnp.full((rows, 1), NEG, jnp.float32),
            jnp.zeros((rows, 1), jnp.float32),
            jnp.zeros((rows, head_dim), jnp.float32),
        )
        for _ in items
    )
    if isinstance(trips, int) and trips == 1:
        return body(0, init)
    return lax.fori_loop(0, trips, body, init)


def cache_kernel(order, live, q_ref, k_hbm, v_hbm, out_ref, kbuf, vbuf, sems,
                 *, sub, kv_shift, g_shift, scale):
    reqs, rows, head_dim = q_ref.shape
    group = kbuf.shape[1]
    flat_len = kbuf.shape[2]
    sub_rows = sub << kv_shift
    subs = flat_len // sub_rows
    lanes = out_ref.shape[2]
    local_len = flat_len >> kv_shift

    small = min(sub, local_len)
    mid = min(2 * sub, local_len)
    big = min(4 * sub, local_len)

    def group_of(first):
        members = [order[first + member] for member in range(group)]
        counts = [live[req] for req in members]
        top = counts[0]
        for count in counts[1:]:
            top = jnp.maximum(top, count)
        span = jnp.where(top <= small, small, jnp.where(top <= mid, mid, ((top + big - 1) // big) * big))
        span = jnp.where(top > 0, span, 0)
        return members, counts, top, span

    def copies(first, slot):
        members, _, _, span = group_of(first)
        out = []
        for member in range(group):
            for c in range(subs):
                window = pl.ds(c * sub_rows, sub_rows)
                out.append((
                    c * sub < span,
                    pltpu.make_async_copy(k_hbm.at[members[member], window, :],
                                          kbuf.at[slot, member, window, :], sems.at[slot, member, 0, c]),
                    pltpu.make_async_copy(v_hbm.at[members[member], window, :],
                                          vbuf.at[slot, member, window, :], sems.at[slot, member, 1, c]),
                ))
        return out

    def start(first, slot):
        for needed, kc, vc in copies(first, slot):
            @pl.when(needed)
            def _():
                kc.start()
                vc.start()

    def wait(first, slot):
        for needed, kc, vc in copies(first, slot):
            @pl.when(needed)
            def _():
                kc.wait()
                vc.wait()

    start(0, 0)

    def per_group(index, carry):
        slot = index % 2
        first = index * group

        @pl.when(first + group < reqs)
        def _():
            start(first + group, 1 - slot)

        wait(first, slot)
        members, counts, top, _ = group_of(first)
        items = [
            (q_ref[members[member]], kbuf.at[slot, member], vbuf.at[slot, member], counts[member])
            for member in range(group)
        ]

        def finish(results):
            per_row = lanes // rows
            stat_count = 5
            stat_rows = (stat_count + per_row - 1) // per_row
            lane = lax.broadcasted_iota(jnp.int32, (rows, lanes), 1)
            blocks = [jnp.zeros((rows, lanes), jnp.float32) for _ in range(per_row)]
            for member, (m, l, acc) in enumerate(results):
                alive = counts[member] > 0
                m = jnp.where(alive, m, NEG)
                l = jnp.where(alive, l, 0.0)
                acc = jnp.where(alive, acc / jnp.where(alive, l, 1.0), 0.0)
                out_ref[members[member], :rows, :] = acc.astype(out_ref.dtype)
                vectors = split_pieces(m, 3) + split_pieces(l, 2)
                for k, vector in enumerate(vectors):
                    blocks[k % per_row] = jnp.where(
                        lane == member * stat_rows + k // per_row, vector, blocks[k % per_row]
                    )
            if lanes > rows * per_row:
                blocks.append(jnp.zeros((lanes - rows * per_row, lanes), jnp.float32))
            flipped = jnp.transpose(jnp.concatenate(blocks, axis=0))
            pad = jnp.zeros((out_ref.shape[1] - rows - stat_rows, lanes), jnp.float32)
            for member in range(len(results)):
                mine = flipped[member * stat_rows:(member + 1) * stat_rows, :]
                out_ref[members[member], rows:, :] = jnp.concatenate([mine, pad], axis=0).astype(out_ref.dtype)

        @pl.when(top == 0)
        def _():
            finish([
                (
                    jnp.full((rows, 1), NEG, jnp.float32),
                    jnp.zeros((rows, 1), jnp.float32),
                    jnp.zeros((rows, head_dim), jnp.float32),
                )
                for _ in range(group)
            ])

        @pl.when((top > 0) & (top <= small))
        def _():
            finish(attend_chunks(items, small, 1, kv_shift, g_shift, scale))

        @pl.when((top > small) & (top <= mid))
        def _():
            finish(attend_chunks(items, mid, 1, kv_shift, g_shift, scale))

        @pl.when(top > mid)
        def _():
            finish(attend_chunks(items, big, (top + big - 1) // big, kv_shift, g_shift, scale))

        return carry

    lax.fori_loop(0, reqs // group, per_group, 0)


def cache_attention(q_blocks, keys, values, live, kv_local, group_size, sub=256, group=4):
    reqs, rows, head_dim = q_blocks.shape
    assert 2 * rows <= head_dim
    flat_len = keys.shape[1]
    local_len = flat_len // kv_local
    sub = min(sub, local_len)
    assert local_len % (4 * sub) == 0 or local_len <= 4 * sub
    group = group if reqs % group == 0 else 1
    kernel = functools.partial(
        cache_kernel,
        sub=sub,
        kv_shift=log2_exact(kv_local),
        g_shift=log2_exact(group_size),
        scale=1.0 / math.sqrt(head_dim),
    )
    ids = jnp.arange(reqs, dtype=jnp.int32)
    sort_key = live * reqs + ids
    rank = jnp.sum((sort_key[None, :] < sort_key[:, None]).astype(jnp.int32), axis=1)
    order = jnp.sum(jnp.where(rank[None, :] == ids[:, None], ids[None, :], 0), axis=1).astype(jnp.int32)
    vmem = pltpu.MemorySpace.VMEM if hasattr(pltpu, "MemorySpace") else pltpu.TPUMemorySpace.VMEM
    return pl.pallas_call(
        kernel,
        in_specs=[
            pl.BlockSpec(memory_space=pltpu.SMEM),
            pl.BlockSpec(memory_space=pltpu.SMEM),
            pl.BlockSpec(memory_space=vmem),
            pl.BlockSpec(memory_space=pl.ANY),
            pl.BlockSpec(memory_space=pl.ANY),
        ],
        out_specs=pl.BlockSpec(memory_space=vmem),
        out_shape=jax.ShapeDtypeStruct((reqs, rows + 16, head_dim), jnp.bfloat16),
        scratch_shapes=[
            pltpu.VMEM((2, group, flat_len, head_dim), keys.dtype),
            pltpu.VMEM((2, group, flat_len, head_dim), values.dtype),
            pltpu.SemaphoreType.DMA((2, group, 2, flat_len // (sub * kv_local))),
        ],
    )(order, live, q_blocks, keys, values)


def project_kernel(tokens_ref, q_ref, k_ref, v_ref, out_ref):
    q_width = q_ref.shape[1]
    k_width = k_ref.shape[1]
    tokens = tokens_ref[...]
    out_ref[:, :q_width] = jnp.dot(tokens, q_ref[...], preferred_element_type=jnp.float32).astype(out_ref.dtype)
    out_ref[:, q_width:q_width + k_width] = jnp.dot(
        tokens, k_ref[...], preferred_element_type=jnp.float32
    ).astype(out_ref.dtype)
    out_ref[:, q_width + k_width:] = jnp.dot(
        tokens, v_ref[...], preferred_element_type=jnp.float32
    ).astype(out_ref.dtype)


def project(tokens, q_weight, key_matrix, value_matrix):
    rows = tokens.shape[0]
    width = q_weight.shape[1] + key_matrix.shape[1] + value_matrix.shape[1]
    vmem = pltpu.MemorySpace.VMEM if hasattr(pltpu, "MemorySpace") else pltpu.TPUMemorySpace.VMEM
    return pl.pallas_call(
        project_kernel,
        in_specs=[pl.BlockSpec(memory_space=vmem)] * 4,
        out_specs=pl.BlockSpec(memory_space=vmem),
        out_shape=jax.ShapeDtypeStruct((rows, width), jnp.bfloat16),
    )(tokens, q_weight, key_matrix, value_matrix)


def halving_sum(part, axis):
    size = lax.axis_size(axis)
    index = lax.axis_index(axis)
    steps = log2_exact(size)
    current = part
    for step in reversed(range(steps)):
        bit = 1 << step
        keep = (index >> step) & 1
        halves = current.reshape((2, current.shape[0] // 2) + current.shape[1:])
        mine = lax.dynamic_index_in_dim(halves, keep, 0, False)
        other = lax.dynamic_index_in_dim(halves, 1 - keep, 0, False)
        if step == steps - 1:
            other = other.astype(jnp.bfloat16)
        received = lax.ppermute(other, axis, [(i, i ^ bit) for i in range(size)])
        current = mine.astype(jnp.float32) + received.astype(jnp.float32)
    return current


def sum_over(part, axis):
    size = lax.axis_size(axis)
    split = part.reshape((size, part.shape[0] // size) + part.shape[1:])
    return jnp.sum(lax.all_to_all(split, axis, 0, 0).astype(jnp.float32), axis=0)


def on_device(
    tokens,
    q_weight,
    key_matrix,
    value_matrix,
    q_gain,
    key_norm_scale,
    stored_cache_keys,
    stored_cache_values,
    lengths,
    positions,
    o_weight,
):
    rows = tokens.shape[0]
    reqs, drafts = positions.shape
    kv_size = lax.axis_size("kv")
    kv_idx = lax.axis_index("kv")
    own_rows = rows // kv_size
    own_reqs = own_rows // drafts
    row0 = kv_idx * own_rows
    kv_local, head_dim = key_norm_scale.shape
    heads_local = q_gain.shape[0]
    group_size = heads_local // kv_local
    q_width = heads_local * head_dim
    k_width = kv_local * head_dim

    proj_own = sum_over(project(tokens, q_weight, key_matrix, value_matrix), "kv")
    pos_own = lax.dynamic_slice_in_dim(positions.reshape(rows), row0, own_rows)
    q_own = norm_rotate(proj_own[:, :q_width], q_gain, pos_own)
    k_own = norm_rotate(proj_own[:, q_width:q_width + k_width], key_norm_scale, pos_own)
    v_own = proj_own[:, q_width + k_width:].astype(jnp.bfloat16)
    rows_r = drafts * heads_local
    q_blocks = lax.all_gather(
        q_own.reshape(own_reqs, rows_r, head_dim), "kv", axis=0, tiled=True
    )

    local_len = stored_cache_keys.shape[1]
    offset = kv_idx * local_len
    live = jnp.clip(lengths - offset, 0, local_len).astype(jnp.int32)
    keys = stored_cache_keys.reshape(reqs, local_len * kv_local, head_dim)
    values = stored_cache_values.reshape(reqs, local_len * kv_local, head_dim)
    partial = cache_attention(q_blocks, keys, values, live, kv_local, group_size)
    gathered = lax.all_to_all(
        partial.reshape((kv_size, own_reqs) + partial.shape[1:]), "kv", 0, 0
    )
    acc_g = gathered[:, :, :rows_r, :].astype(jnp.float32)
    per_row = head_dim // rows_r
    stats = gathered[:, :, rows_r:, :].astype(jnp.float32)

    def stat(k):
        lane0 = (k % per_row) * rows_r
        return stats[:, :, k // per_row, lane0:lane0 + rows_r]

    m_g = stat(0) + stat(1) + stat(2)
    l_g = stat(3) + stat(4)

    scale = 1.0 / math.sqrt(head_dim)
    q_d = q_own.reshape(own_reqs, drafts, kv_local, group_size, head_dim)
    k_d = k_own.reshape(own_reqs, drafts, kv_local, head_dim)
    v_d = v_own.reshape(own_reqs, drafts, kv_local, head_dim)
    s_d = jnp.einsum("rjkgd,rikd->rjkgi", q_d, k_d, preferred_element_type=jnp.float32) * scale
    pos_req = lax.dynamic_slice_in_dim(positions, kv_idx * own_reqs, own_reqs)
    order = jnp.arange(drafts, dtype=jnp.int32)
    seen = (order[None, :] == order[:, None])[None] | (order[None, :] < order[:, None])[None] & (
        pos_req[:, None, :] < pos_req[:, :, None]
    )
    mask_d = seen[:, :, None, None, :]
    s_d = jnp.where(mask_d, s_d, NEG)
    m_d = jnp.max(s_d, axis=-1)
    p_d = jnp.where(mask_d, jnp.exp(s_d - m_d[..., None]), 0.0)
    l_d = jnp.sum(p_d, axis=-1).reshape(own_reqs, rows_r)
    acc_d = jnp.einsum(
        "rjkgi,rikd->rjkgd", p_d.astype(jnp.bfloat16), v_d, preferred_element_type=jnp.float32
    ).reshape(own_reqs, rows_r, head_dim)
    m_d = m_d.reshape(own_reqs, rows_r)

    top = jnp.maximum(jnp.max(m_g, axis=0), m_d)
    ratio = jnp.exp(m_g - top[None]) * l_g
    ratio_d = jnp.exp(m_d - top)
    total = jnp.sum(ratio, axis=0) + l_d * ratio_d
    acc = jnp.sum(acc_g * ratio[..., None], axis=0) + acc_d * ratio_d[..., None]
    attended = (acc / total[..., None]).astype(jnp.bfloat16).reshape(own_rows, q_width)
    attended = lax.all_gather(attended, "kv", axis=0, tiled=True)
    partial_out = jnp.dot(attended, o_weight, preferred_element_type=jnp.float32)
    return halving_sum(partial_out, "head").astype(jnp.bfloat16)


def solution(mesh):
    placed = (
        P(None, "kv"),
        P("kv", "head"),
        P("kv", "head"),
        P("kv", "head"),
        P("head", None),
        P("head", None),
        P(None, "kv", "head", None),
        P(None, "kv", "head", None),
        P(),
        P(),
        P("head", "kv"),
    )
    return jax.shard_map(
        on_device, mesh=mesh, in_specs=placed, out_specs=P("head", "kv"), check_vma=False
    )
```
